32 devices in a mesh: dp: 4 (over y, x), seq: 8 (over z, core).
Axes of the slice: x: 2, y: 2, z: 4, core: 2. Of those that a mesh axis runs over, the one named last changes fastest.
Arguments:
- queries: bfloat16 [4, 8, 512, 2048], P('dp', 'seq'), may hold values from -48 to 48
- keys: bfloat16 [4, 8, 512, 2048], P('dp', 'seq'), may hold values from -6 to 6
- values: bfloat16 [4, 8, 512, 2048], P('dp', 'seq'), may hold values from -6 to 6
- out_grad: bfloat16 [4, 8, 512, 2048], P('dp', 'seq'), may hold values from -6 to 6
- out_weight: bfloat16 [2048, 2048], P('dp'), may hold values from -0.125 to 0.125
- row_mask: int32 [4, 4], replicated, may hold values from 0 to 1, as said below
- col_mask: int32 [8, 8], replicated, may hold values from 0 to 1, as said below
Outputs:
- layer_out: bfloat16 [4, 8, 512, 2048], P('dp', 'seq')
- query_grad: bfloat16 [4, 8, 512, 2048], P('dp', 'seq')
- key_grad: bfloat16 [4, 8, 512, 2048], P('dp', 'seq')
- value_grad: bfloat16 [4, 8, 512, 2048], P('dp', 'seq')
- wo_grad: float32 [2048, 2048], P(('dp', 'seq'))
The draws below stay inside these ranges and needn't reach their ends.
Inputs may be any that keep to these rules, and one draw needn't show every extreme that they name: row_mask[a, b] is 1 for b = a and 0 for b > a. col_mask[r, s] is 1 for s = r and for s = r - 1, and 0 for s > r.
All inputs are finite; a program needn't handle non-finite values.
Results may differ from the reference program's by a relative error of at most 0.012.
Values may be sent and summed in bfloat16 or wider, within the bound.
No kernel may reach another device: no remote copies, remote signals or barrier semaphores. Data moves between devices by JAX's collectives and lax.ppermute only.
A program may use at most 192 MiB of HBM per device.

```python
import math
import jax
import jax.numpy as jnp
from jax import lax

D = 2048
DH = 128
COLS = 512
BLK = 128
SEQS = 4
ROWS = 8
NBLK = 4
TOTAL = 16384


def paired_draw(key):
    first = jax.random.fold_in(key, 11)
    second = jax.random.fold_in(key, 23)
    full_shape = (SEQS, ROWS, COLS, D)
    queries_out = jnp.clip(jax.random.normal(first, full_shape, jnp.float32), -6.0, 6.0)
    keys_out = jnp.clip(jax.random.normal(second, full_shape, jnp.float32), -6.0, 6.0)
    return (queries_out, keys_out)


def draw_queries(key, part):
    return paired_draw(key)[0].astype(jnp.bfloat16)


def draw_keys(key, part):
    return paired_draw(key)[1].astype(jnp.bfloat16)


def draw_row_mask(key, part):
    random_bits = jax.random.randint(key, (NBLK, NBLK), 0, 2)
    row_index = lax.broadcasted_iota(jnp.int32, (NBLK, NBLK), 0)
    col_index = lax.broadcasted_iota(jnp.int32, (NBLK, NBLK), 1)
    return jnp.where(col_index < row_index, random_bits, jnp.where(col_index == row_index, 1, 0)).astype(jnp.int32)


def draw_col_mask(key, part):
    random_bits = jax.random.randint(key, (ROWS, ROWS), 0, 2)
    row_index = lax.broadcasted_iota(jnp.int32, (ROWS, ROWS), 0)
    col_index = lax.broadcasted_iota(jnp.int32, (ROWS, ROWS), 1)
    near = (col_index == row_index) | (col_index == row_index - 1)
    return jnp.where(near, 1, jnp.where(col_index < row_index - 1, random_bits, 0)).astype(jnp.int32)


def spiked(values, key, source, target, parts, factor):
    owner, partner = [(jnp.arange(values.shape[dim]) // (values.shape[dim] // parts)).reshape([-1 if axis == dim else 1 for axis in range(values.ndim)]) for dim in (source, target)]
    chosen = jax.random.permutation(key, parts)[partner]
    strong = (owner == chosen) | (owner == (partner + parts // 2) % parts)
    return jnp.where(strong, factor * values, values)


def levels(rng, dims, shards, low, high):
    def one(position, shards_of):
        heights = jax.random.uniform(jax.random.fold_in(jax.random.fold_in(rng, 6), position), (shards_of,), jnp.float32, low / len(shards), high / len(shards))
        return jnp.repeat(jnp.exp(heights), dims[position] // shards_of).reshape((-1,) + (1,) * (len(dims) - position - 1))

    gain = one(*shards[0])
    for cut in shards[1:]:
        gain = gain * one(*cut)
    return gain


def bell_draw(key, dims, deviation, bound, pieces=(), held_as=jnp.bfloat16):
    entries = deviation * jax.random.normal(key, dims, jnp.float32)
    if pieces:
        entries = entries * levels(key, dims, pieces, -0.22, 0.18)
    return jnp.clip(entries, -bound, bound).astype(held_as)


def heavy_noise(key, extent, scale, limit, shards, heavy, kind=jnp.bfloat16):
    values = scale * jax.random.normal(key, extent, jnp.float32)
    if shards:
        values = values * levels(key, extent, shards, -0.22, 0.18)
    return jnp.clip(spiked(values, jax.random.fold_in(key, 3), *heavy), -limit, limit).astype(kind)


def setup_inputs(seed: int = 0) -> dict:
    streams_of = jax.random.split(jax.random.key(seed), 8)
    return {
        "queries": draw_queries(jax.random.fold_in(streams_of[7], 71), 0),
        "keys": draw_keys(jax.random.fold_in(streams_of[7], 71), 0),
        "values": bell_draw(streams_of[2], (SEQS, ROWS, COLS, D), 1.0, 6.0, ((0, 4), (1, 8))),
        "out_grad": heavy_noise(streams_of[3], (SEQS, ROWS, COLS, D), 1.0, 6.0, ((0, 4), (1, 8)), (1, 3, 8, 2.0)),
        "out_weight": bell_draw(streams_of[4], (D, D), D ** -0.5, 0.125, ((0, 4),)),
        "row_mask": draw_row_mask(jax.random.fold_in(streams_of[7], 71), 0),
        "col_mask": draw_col_mask(jax.random.fold_in(streams_of[7], 71), 0),
    }


masked_out = -1e+30

def wide(tensor):
    return tensor.astype(jnp.float32)

def narrow(tensor):
    return lax.optimization_barrier(tensor.astype(jnp.bfloat16)).astype(jnp.float32)

def stored(tensor):
    return lax.optimization_barrier(tensor.astype(jnp.bfloat16))

def split_heads(tensor):
    return wide(tensor).reshape(tensor.shape[:3] + (tensor.shape[3] // DH, DH))

def row_permit(row_mask):
    spread = jnp.repeat(jnp.repeat(row_mask, BLK, axis=0), BLK, axis=1)
    row_index = lax.broadcasted_iota(jnp.int32, (COLS, COLS), 0)
    col_index = lax.broadcasted_iota(jnp.int32, (COLS, COLS), 1)
    return (spread == 1) & (col_index <= row_index)

def row_scores(queries, keys):
    return jnp.einsum('brihd,brjhd->brhij', split_heads(queries), split_heads(keys)) * (1.0 / math.sqrt(DH))

def column_scores(queries, keys):
    return jnp.einsum('brchd,bschd->bchrs', split_heads(queries), split_heads(keys)) * (1.0 / math.sqrt(DH))

def row_forward(queries, keys, values, allowed):
    scores = row_scores(queries, keys)
    highest = lax.optimization_barrier(jnp.max(jnp.where(allowed, scores, masked_out), axis=-1, keepdims=True))
    attend = jnp.exp(jnp.where(allowed, scores - highest, masked_out))
    totals = lax.optimization_barrier(jnp.sum(attend, axis=-1, keepdims=True))
    probs = narrow(attend / totals)
    output = jnp.einsum('brhij,brjhd->brihd', probs, split_heads(values))
    log_total = jnp.transpose((highest + jnp.log(totals))[..., 0], (0, 1, 3, 2))
    return (stored(output.reshape(queries.shape)), log_total)

def column_forward(queries, keys, values, allowed):
    scores = column_scores(queries, keys)
    highest = lax.optimization_barrier(jnp.max(jnp.where(allowed, scores, masked_out), axis=-1, keepdims=True))
    attend = jnp.exp(jnp.where(allowed, scores - highest, masked_out))
    totals = lax.optimization_barrier(jnp.sum(attend, axis=-1, keepdims=True))
    probs = narrow(attend / totals)
    output = jnp.einsum('bchrs,bschd->brchd', probs, split_heads(values))
    log_total = jnp.transpose((highest + jnp.log(totals))[..., 0], (0, 3, 1, 2))
    return (stored(output.reshape(queries.shape)), log_total)

def row_backward(queries, keys, values, output, grads, log_total, allowed):
    scale = 1.0 / math.sqrt(DH)
    query_heads, key_heads, value_heads = (split_heads(queries), split_heads(keys), split_heads(values))
    out_heads, grad_heads = (split_heads(output), split_heads(grads))
    grad_dot = jnp.einsum('brihd,brihd->brhi', grad_heads, out_heads)
    scores = row_scores(queries, keys)
    attend = jnp.exp(jnp.where(allowed, scores - jnp.transpose(log_total, (0, 1, 3, 2))[..., None], masked_out))
    value_grad = jnp.einsum('brhij,brihd->brjhd', narrow(attend), grad_heads)
    attend_grad = jnp.einsum('brihd,brjhd->brhij', grad_heads, value_heads)
    score_grad = narrow(attend * (attend_grad - grad_dot[..., None]))
    query_grad = jnp.einsum('brhij,brjhd->brihd', score_grad, key_heads) * scale
    key_grad = jnp.einsum('brhij,brihd->brjhd', score_grad, query_heads) * scale
    return tuple((gradient.reshape(queries.shape).astype(jnp.bfloat16) for gradient in (query_grad, key_grad, value_grad)))

def column_backward(queries, keys, values, output, grads, log_total, allowed):
    scale = 1.0 / math.sqrt(DH)
    query_heads, key_heads, value_heads = (split_heads(queries), split_heads(keys), split_heads(values))
    out_heads, grad_heads = (split_heads(output), split_heads(grads))
    grad_dot = jnp.einsum('brchd,brchd->bchr', grad_heads, out_heads)
    scores = column_scores(queries, keys)
    attend = jnp.exp(jnp.where(allowed, scores - jnp.transpose(log_total, (0, 2, 3, 1))[..., None], masked_out))
    value_grad = jnp.einsum('bchrs,brchd->bschd', narrow(attend), grad_heads)
    attend_grad = jnp.einsum('brchd,bschd->bchrs', grad_heads, value_heads)
    score_grad = narrow(attend * (attend_grad - grad_dot[..., None]))
    query_grad = jnp.einsum('bchrs,bschd->brchd', score_grad, key_heads) * scale
    key_grad = jnp.einsum('bchrs,brchd->bschd', score_grad, query_heads) * scale
    return tuple((gradient.reshape(queries.shape).astype(jnp.bfloat16) for gradient in (query_grad, key_grad, value_grad)))

def reference(queries, keys, values, out_grad, out_weight, row_mask, col_mask):
    half_width = D // 2
    row_ok = row_permit(row_mask)
    col_ok = col_mask == 1

    def by_rows(tensor):
        return tensor[..., :half_width].reshape(SEQS * ROWS, 1, 1, COLS, half_width)

    def by_columns(tensor):
        return tensor[..., half_width:].reshape(SEQS, 1, ROWS, COLS, half_width)

    def whole(tensor):
        return tensor.reshape(SEQS, ROWS, COLS, half_width)
    row_in = (by_rows(queries), by_rows(keys), by_rows(values))
    col_in = (by_columns(queries), by_columns(keys), by_columns(values))
    row_out, row_total = lax.map(lambda packed: row_forward(packed[0], packed[1], packed[2], row_ok), row_in)
    column_out, column_total = lax.map(lambda packed: column_forward(packed[0], packed[1], packed[2], col_ok), col_in)
    attention = jnp.concatenate([whole(row_out), whole(column_out)], axis=3)
    flat_attn = attention.reshape(-1, D)
    flat_grad = out_grad.reshape(-1, D)
    layer_out = jnp.dot(flat_attn, out_weight, preferred_element_type=jnp.float32).astype(jnp.bfloat16).reshape(queries.shape)
    attn_grad = stored(jnp.dot(flat_grad, out_weight.T, preferred_element_type=jnp.float32)).reshape(queries.shape)
    wo_grad = jnp.dot(flat_attn.T, flat_grad, preferred_element_type=jnp.float32) * (1.0 / math.sqrt(TOTAL))
    row_grads = lax.map(lambda packed: row_backward(*packed, row_ok), row_in + (row_out, by_rows(attn_grad), row_total))
    column_grads = lax.map(lambda packed: column_backward(*packed, col_ok), col_in + (column_out, by_columns(attn_grad), column_total))
    grads = [jnp.concatenate([whole(row_grads[member]), whole(column_grads[member])], axis=3) for member in range(3)]
    return (layer_out, grads[0], grads[1], grads[2], wo_grad)
```

```python
import math

import jax
import jax.numpy as jnp
from jax import lax
from jax.sharding import PartitionSpec as P

DH = 128
COLS = 512
BLK = 128

masked_out = -1e30
scale = 1.0 / math.sqrt(DH)


def row_permit(row_mask):
    spread = jnp.repeat(jnp.repeat(row_mask, BLK, axis=0), BLK, axis=1)
    row_index = lax.broadcasted_iota(jnp.int32, (COLS, COLS), 0)
    col_index = lax.broadcasted_iota(jnp.int32, (COLS, COLS), 1)
    return (spread == 1) & (col_index <= row_index)


def softmax_parts(scores, allowed):
    highest = jnp.max(jnp.where(allowed, scores, masked_out), axis=-1, keepdims=True)
    attend = jnp.exp(jnp.where(allowed, scores - highest, masked_out))
    totals = jnp.sum(attend, axis=-1, keepdims=True)
    probs = (attend / totals).astype(jnp.bfloat16)
    return probs, highest + jnp.log(totals)


def row_forward(q, k, v, allowed):
    scores = jnp.einsum("ihd,jhd->hij", q, k, preferred_element_type=jnp.float32) * scale
    probs, log_total = softmax_parts(scores, allowed[None])
    out = jnp.einsum("hij,jhd->ihd", probs, v, preferred_element_type=jnp.float32)
    return out.astype(jnp.bfloat16), scores, log_total


def row_backward(q, k, v, out, grad, scores, log_total, allowed):
    grad_dot = jnp.einsum("ihd,ihd->hi", grad, out, preferred_element_type=jnp.float32)
    back = jnp.where(allowed[None], jnp.exp(scores - log_total), 0.0)
    value_grad = jnp.einsum(
        "hij,ihd->jhd", back.astype(jnp.bfloat16), grad, preferred_element_type=jnp.float32
    )
    prob_grad = jnp.einsum("ihd,jhd->hij", grad, v, preferred_element_type=jnp.float32)
    score_grad = (back * (prob_grad - grad_dot[..., None])).astype(jnp.bfloat16)
    query_grad = jnp.einsum("hij,jhd->ihd", score_grad, k, preferred_element_type=jnp.float32)
    key_grad = jnp.einsum("hij,ihd->jhd", score_grad, q, preferred_element_type=jnp.float32)
    return tuple(
        g.astype(jnp.bfloat16) for g in (query_grad * scale, key_grad * scale, value_grad)
    )


def column_forward(q, k, v, allowed):
    scores = jnp.einsum("rchd,schd->chrs", q, k, preferred_element_type=jnp.float32) * scale
    probs, log_total = softmax_parts(scores, allowed)
    out = jnp.einsum("chrs,schd->rchd", probs, v, preferred_element_type=jnp.float32)
    return out.astype(jnp.bfloat16), scores, log_total


def column_backward(q, k, v, out, grad, scores, log_total, allowed):
    grad_dot = jnp.einsum("rchd,rchd->chr", grad, out, preferred_element_type=jnp.float32)
    back = jnp.where(allowed, jnp.exp(scores - log_total), 0.0)
    value_grad = jnp.einsum(
        "chrs,rchd->schd", back.astype(jnp.bfloat16), grad, preferred_element_type=jnp.float32
    )
    prob_grad = jnp.einsum("rchd,schd->chrs", grad, v, preferred_element_type=jnp.float32)
    score_grad = (back * (prob_grad - grad_dot[..., None])).astype(jnp.bfloat16)
    query_grad = jnp.einsum("chrs,schd->rchd", score_grad, k, preferred_element_type=jnp.float32)
    key_grad = jnp.einsum("chrs,rchd->schd", score_grad, q, preferred_element_type=jnp.float32)
    return tuple(
        g.astype(jnp.bfloat16) for g in (query_grad * scale, key_grad * scale, value_grad)
    )


def on_device(queries, keys, values, out_grad, out_weight, row_mask, col_mask):
    tokens, features = queries.shape[2], queries.shape[3]
    half = features // 2
    heads_half = half // DH
    rows = lax.axis_size("seq")
    cols_each = tokens // rows

    weight = lax.all_gather(out_weight, "dp", axis=0, tiled=True)

    packed = jnp.stack([t[0, 0, :, half:] for t in (queries, keys, values)])
    shipped = lax.all_to_all(packed[None], "seq", split_axis=2, concat_axis=0, tiled=True)
    col_q, col_k, col_v = (
        shipped[:, i].reshape(rows, cols_each, heads_half, DH) for i in range(3)
    )
    col_ok = col_mask == 1
    col_out, col_scores, col_total = column_forward(col_q, col_k, col_v, col_ok)
    col_back = lax.all_to_all(
        col_out.reshape(rows, cols_each, half), "seq", split_axis=0, concat_axis=1, tiled=True
    )

    row_ok = row_permit(row_mask)
    split = lambda t: t[0, 0, :, :half].reshape(tokens, heads_half, DH)
    row_q, row_k, row_v = split(queries), split(keys), split(values)
    row_out, row_scores, row_total = row_forward(row_q, row_k, row_v, row_ok)

    flat_grad = out_grad[0, 0]
    attn_grad = lax.dot_general(
        flat_grad, weight, (((1,), (1,)), ((), ())), preferred_element_type=jnp.float32
    ).astype(jnp.bfloat16)
    grad_cols = lax.all_to_all(
        attn_grad[None, :, half:], "seq", split_axis=1, concat_axis=0, tiled=True
    ).reshape(rows, cols_each, heads_half, DH)
    col_grads = column_backward(
        col_q, col_k, col_v, col_out, grad_cols, col_scores, col_total, col_ok
    )
    col_grads_back = lax.all_to_all(
        jnp.stack([g.reshape(rows, cols_each, half) for g in col_grads]),
        "seq",
        split_axis=1,
        concat_axis=2,
        tiled=True,
    )

    row_grads = row_backward(
        row_q,
        row_k,
        row_v,
        row_out,
        attn_grad[:, :half].reshape(tokens, heads_half, DH),
        row_scores,
        row_total,
        row_ok,
    )

    attention = jnp.concatenate([row_out.reshape(tokens, half), col_back[0]], axis=1)
    layer_out = jnp.dot(attention, weight, preferred_element_type=jnp.float32).astype(
        jnp.bfloat16
    )

    devices_all = lax.axis_size(("dp", "seq"))
    partial = lax.dot_general(
        attention, flat_grad, (((0,), (0,)), ((), ())), preferred_element_type=jnp.float32
    )
    wo_grad = lax.psum_scatter(partial, ("dp", "seq"), scatter_dimension=0, tiled=True) * (
        1.0 / math.sqrt(tokens * devices_all)
    )

    grads = [
        jnp.concatenate([row_grads[i].reshape(tokens, half), col_grads_back[i, 0]], axis=1)[
            None, None
        ]
        for i in range(3)
    ]
    return (layer_out[None, None], grads[0], grads[1], grads[2], wo_grad)


def solution(mesh):
    in_specs = (
        P("dp", "seq", None, None),
        P("dp", "seq", None, None),
        P("dp", "seq", None, None),
        P("dp", "seq", None, None),
        P("dp", None),
        P(),
        P(),
    )
    out_specs = (
        P("dp", "seq", None, None),
        P("dp", "seq", None, None),
        P("dp", "seq", None, None),
        P("dp", "seq", None, None),
        P(("dp", "seq"), None),
    )
    return jax.shard_map(
        on_device, mesh=mesh, in_specs=in_specs, out_specs=out_specs, check_vma=False
    )
```

```python
import math

import jax
import jax.numpy as jnp
from jax import lax
from jax.sharding import PartitionSpec as P

DH = 128
COLS = 512
BLK = 128

masked_out = -1e30
scale = 1.0 / math.sqrt(DH)


def row_permit(row_mask):
    spread = jnp.repeat(jnp.repeat(row_mask, BLK, axis=0), BLK, axis=1)
    row_index = lax.broadcasted_iota(jnp.int32, (COLS, COLS), 0)
    col_index = lax.broadcasted_iota(jnp.int32, (COLS, COLS), 1)
    return (spread == 1) & (col_index <= row_index)


def softmax_parts(scores, allowed):
    highest = jnp.max(jnp.where(allowed, scores, masked_out), axis=-1, keepdims=True)
    attend = jnp.exp(jnp.where(allowed, scores - highest, masked_out))
    totals = jnp.sum(attend, axis=-1, keepdims=True)
    probs = (attend / totals).astype(jnp.bfloat16)
    return probs, highest + jnp.log(totals)


def row_forward(q, k, v, allowed):
    scores = jnp.einsum("ihd,jhd->hij", q, k, preferred_element_type=jnp.float32) * scale
    probs, log_total = softmax_parts(scores, allowed[None])
    out = jnp.einsum("hij,jhd->ihd", probs, v, preferred_element_type=jnp.float32)
    return out.astype(jnp.bfloat16), scores, log_total


def row_backward(q, k, v, out, grad, scores, log_total, allowed):
    grad_dot = jnp.einsum("ihd,ihd->hi", grad, out, preferred_element_type=jnp.float32)
    back = jnp.where(allowed[None], jnp.exp(scores - log_total), 0.0)
    value_grad = jnp.einsum(
        "hij,ihd->jhd", back.astype(jnp.bfloat16), grad, preferred_element_type=jnp.float32
    )
    prob_grad = jnp.einsum("ihd,jhd->hij", grad, v, preferred_element_type=jnp.float32)
    score_grad = (back * (prob_grad - grad_dot[..., None])).astype(jnp.bfloat16)
    query_grad = jnp.einsum("hij,jhd->ihd", score_grad, k, preferred_element_type=jnp.float32)
    key_grad = jnp.einsum("hij,ihd->jhd", score_grad, q, preferred_element_type=jnp.float32)
    return tuple(
        g.astype(jnp.bfloat16) for g in (query_grad * scale, key_grad * scale, value_grad)
    )


def column_forward(q, k, v, allowed):
    scores = jnp.einsum("rchd,schd->chrs", q, k, preferred_element_type=jnp.float32) * scale
    probs, log_total = softmax_parts(scores, allowed)
    out = jnp.einsum("chrs,schd->rchd", probs, v, preferred_element_type=jnp.float32)
    return out.astype(jnp.bfloat16), scores, log_total


def column_backward(q, k, v, out, grad, scores, log_total, allowed):
    grad_dot = jnp.einsum("rchd,rchd->chr", grad, out, preferred_element_type=jnp.float32)
    back = jnp.where(allowed, jnp.exp(scores - log_total), 0.0)
    value_grad = jnp.einsum(
        "chrs,rchd->schd", back.astype(jnp.bfloat16), grad, preferred_element_type=jnp.float32
    )
    prob_grad = jnp.einsum("rchd,schd->chrs", grad, v, preferred_element_type=jnp.float32)
    score_grad = (back * (prob_grad - grad_dot[..., None])).astype(jnp.bfloat16)
    query_grad = jnp.einsum("chrs,schd->rchd", score_grad, k, preferred_element_type=jnp.float32)
    key_grad = jnp.einsum("chrs,rchd->schd", score_grad, q, preferred_element_type=jnp.float32)
    return tuple(
        g.astype(jnp.bfloat16) for g in (query_grad * scale, key_grad * scale, value_grad)
    )


def on_device(queries, keys, values, out_grad, out_weight, row_mask, col_mask):
    tokens, features = queries.shape[2], queries.shape[3]
    half = features // 2
    heads_half = half // DH
    rows = lax.axis_size("seq")
    cols_each = tokens // rows
    core = lax.axis_index("seq") % 2
    pairs = [(2 * m + j, 2 * m + 1 - j) for m in range(rows // 2) for j in range(2)]

    local_rows = out_weight.shape[0]
    mine = lax.dynamic_slice_in_dim(out_weight, core * (local_rows // 2), local_rows // 2)
    gathered = lax.all_gather(mine, "dp", axis=0, tiled=False)
    theirs = lax.ppermute(gathered, "seq", pairs)
    weight = jnp.where(
        core == 0, jnp.stack([gathered, theirs], axis=1), jnp.stack([theirs, gathered], axis=1)
    ).reshape(features, features)
    grad_mate = lax.ppermute(out_grad[0, 0], "seq", pairs)

    packed = jnp.stack([t[0, 0, :, half:] for t in (queries, keys, values)])
    shipped = lax.all_to_all(packed[None], "seq", split_axis=2, concat_axis=0, tiled=True)
    col_q, col_k, col_v = (
        shipped[:, i].reshape(rows, cols_each, heads_half, DH) for i in range(3)
    )
    col_ok = col_mask == 1
    col_out, col_scores, col_total = column_forward(col_q, col_k, col_v, col_ok)
    col_back = lax.all_to_all(
        col_out.reshape(rows, cols_each, half), "seq", split_axis=0, concat_axis=1, tiled=True
    )

    row_ok = row_permit(row_mask)
    split = lambda t: t[0, 0, :, :half].reshape(tokens, heads_half, DH)
    row_q, row_k, row_v = split(queries), split(keys), split(values)
    row_out, row_scores, row_total = row_forward(row_q, row_k, row_v, row_ok)

    flat_grad = out_grad[0, 0]
    attn_grad = lax.dot_general(
        flat_grad, weight, (((1,), (1,)), ((), ())), preferred_element_type=jnp.float32
    ).astype(jnp.bfloat16)
    grad_cols = lax.all_to_all(
        attn_grad[None, :, half:], "seq", split_axis=1, concat_axis=0, tiled=True
    ).reshape(rows, cols_each, heads_half, DH)
    col_grads = column_backward(
        col_q, col_k, col_v, col_out, grad_cols, col_scores, col_total, col_ok
    )
    col_grads_back = lax.all_to_all(
        jnp.stack([g.reshape(rows, cols_each, half) for g in col_grads]),
        "seq",
        split_axis=1,
        concat_axis=2,
        tiled=True,
    )

    row_grads = row_backward(
        row_q,
        row_k,
        row_v,
        row_out,
        attn_grad[:, :half].reshape(tokens, heads_half, DH),
        row_scores,
        row_total,
        row_ok,
    )

    attention = jnp.concatenate([row_out.reshape(tokens, half), col_back[0]], axis=1)
    layer_out = jnp.dot(attention, weight, preferred_element_type=jnp.float32).astype(
        jnp.bfloat16
    )

    block = local_rows // rows
    by_parity = attention.reshape(tokens, features // (2 * block), 2, block)
    own_rows = jnp.where(core == 0, by_parity[:, :, 0], by_parity[:, :, 1])
    mate_rows = lax.ppermute(
        jnp.where(core == 0, by_parity[:, :, 1], by_parity[:, :, 0]), "seq", pairs
    )
    pair_attn = jnp.concatenate([own_rows, mate_rows], axis=0).reshape(2 * tokens, features // 2)
    pair_grad = jnp.concatenate([flat_grad, grad_mate], axis=0)
    partial = lax.dot_general(
        pair_attn, pair_grad, (((0,), (0,)), ((), ())), preferred_element_type=jnp.float32
    )
    dp_size = lax.axis_size("dp")
    devices_all = dp_size * rows
    groups = [
        [d * rows + 2 * m + c for d in range(dp_size) for m in range(rows // 2)] for c in range(2)
    ]
    wo_grad = lax.psum_scatter(
        partial, ("dp", "seq"), scatter_dimension=0, tiled=True, axis_index_groups=groups
    ) * (1.0 / math.sqrt(tokens * devices_all))

    grads = [
        jnp.concatenate([row_grads[i].reshape(tokens, half), col_grads_back[i, 0]], axis=1)[
            None, None
        ]
        for i in range(3)
    ]
    return (layer_out[None, None], grads[0], grads[1], grads[2], wo_grad)


def solution(mesh):
    in_specs = (
        P("dp", "seq", None, None),
        P("dp", "seq", None, None),
        P("dp", "seq", None, None),
        P("dp", "seq", None, None),
        P("dp", None),
        P(),
        P(),
    )
    out_specs = (
        P("dp", "seq", None, None),
        P("dp", "seq", None, None),
        P("dp", "seq", None, None),
        P("dp", "seq", None, None),
        P(("dp", "seq"), None),
    )
    return jax.shard_map(
        on_device, mesh=mesh, in_specs=in_specs, out_specs=out_specs, check_vma=False
    )
```

```python
import math

import jax
import jax.numpy as jnp
from jax import lax
from jax.sharding import PartitionSpec as P

DH = 128
COLS = 512
BLK = 128

masked_out = -1e30
scale = 1.0 / math.sqrt(DH)


def row_permit(row_mask):
    spread = jnp.repeat(jnp.repeat(row_mask, BLK, axis=0), BLK, axis=1)
    row_index = lax.broadcasted_iota(jnp.int32, (COLS, COLS), 0)
    col_index = lax.broadcasted_iota(jnp.int32, (COLS, COLS), 1)
    return (spread == 1) & (col_index <= row_index)


def softmax_parts(scores, allowed):
    highest = jnp.max(jnp.where(allowed, scores, masked_out), axis=-1, keepdims=True)
    attend = jnp.exp(jnp.where(allowed, scores - highest, masked_out))
    totals = jnp.sum(attend, axis=-1, keepdims=True)
    probs = (attend / totals).astype(jnp.bfloat16)
    return probs, highest + jnp.log(totals)


def row_forward(q, k, v, allowed):
    scores = jnp.einsum("ihd,jhd->hij", q, k, preferred_element_type=jnp.float32) * scale
    probs, log_total = softmax_parts(scores, allowed[None])
    out = jnp.einsum("hij,jhd->ihd", probs, v, preferred_element_type=jnp.float32)
    return out.astype(jnp.bfloat16), scores, log_total


def row_backward(q, k, v, out, grad, scores, log_total, allowed):
    grad_dot = jnp.einsum("ihd,ihd->hi", grad, out, preferred_element_type=jnp.float32)
    back = jnp.where(allowed[None], jnp.exp(scores - log_total), 0.0)
    value_grad = jnp.einsum(
        "hij,ihd->jhd", back.astype(jnp.bfloat16), grad, preferred_element_type=jnp.float32
    )
    prob_grad = jnp.einsum("ihd,jhd->hij", grad, v, preferred_element_type=jnp.float32)
    score_grad = (back * (prob_grad - grad_dot[..., None])).astype(jnp.bfloat16)
    query_grad = jnp.einsum("hij,jhd->ihd", score_grad, k, preferred_element_type=jnp.float32)
    key_grad = jnp.einsum("hij,ihd->jhd", score_grad, q, preferred_element_type=jnp.float32)
    return tuple(
        g.astype(jnp.bfloat16) for g in (query_grad * scale, key_grad * scale, value_grad)
    )


def column_forward(q, k, v, allowed):
    scores = jnp.einsum("rchd,schd->chrs", q, k, preferred_element_type=jnp.float32) * scale
    probs, log_total = softmax_parts(scores, allowed)
    out = jnp.einsum("chrs,schd->rchd", probs, v, preferred_element_type=jnp.float32)
    return out.astype(jnp.bfloat16), scores, log_total


def column_backward(q, k, v, out, grad, scores, log_total, allowed):
    grad_dot = jnp.einsum("rchd,rchd->chr", grad, out, preferred_element_type=jnp.float32)
    back = jnp.where(allowed, jnp.exp(scores - log_total), 0.0)
    value_grad = jnp.einsum(
        "chrs,rchd->schd", back.astype(jnp.bfloat16), grad, preferred_element_type=jnp.float32
    )
    prob_grad = jnp.einsum("rchd,schd->chrs", grad, v, preferred_element_type=jnp.float32)
    score_grad = (back * (prob_grad - grad_dot[..., None])).astype(jnp.bfloat16)
    query_grad = jnp.einsum("chrs,schd->rchd", score_grad, k, preferred_element_type=jnp.float32)
    key_grad = jnp.einsum("chrs,rchd->schd", score_grad, q, preferred_element_type=jnp.float32)
    return tuple(
        g.astype(jnp.bfloat16) for g in (query_grad * scale, key_grad * scale, value_grad)
    )


def on_device(queries, keys, values, out_grad, out_weight, row_mask, col_mask):
    tokens, features = queries.shape[2], queries.shape[3]
    half = features // 2
    heads_half = half // DH
    rows = lax.axis_size("seq")
    cols_each = tokens // rows

    weight = lax.all_gather(out_weight, "dp", axis=0, tiled=True)

    packed = jnp.stack([t[0, 0, :, half:] for t in (queries, keys, values)])
    shipped = lax.all_to_all(packed[None], "seq", split_axis=2, concat_axis=0, tiled=True)
    col_q, col_k, col_v = (
        shipped[:, i].reshape(rows, cols_each, heads_half, DH) for i in range(3)
    )
    col_ok = col_mask == 1
    col_out, col_scores, col_total = column_forward(col_q, col_k, col_v, col_ok)
    col_back = lax.all_to_all(
        col_out.reshape(rows, cols_each, half), "seq", split_axis=0, concat_axis=1, tiled=True
    )

    row_ok = row_permit(row_mask)
    split = lambda t: t[0, 0, :, :half].reshape(tokens, heads_half, DH)
    row_q, row_k, row_v = split(queries), split(keys), split(values)
    row_out, row_scores, row_total = row_forward(row_q, row_k, row_v, row_ok)

    flat_grad = out_grad[0, 0]
    attention = jnp.concatenate([row_out.reshape(tokens, half), col_back[0]], axis=1)
    partial = lax.dot_general(
        attention, flat_grad, (((0,), (0,)), ((), ())), preferred_element_type=jnp.float32
    )
    partial, weight = lax.optimization_barrier((partial, weight))
    devices_all = lax.axis_size(("dp", "seq"))
    wo_grad = lax.psum_scatter(partial, ("dp", "seq"), scatter_dimension=0, tiled=True) * (
        1.0 / math.sqrt(tokens * devices_all)
    )

    attn_grad = lax.dot_general(
        flat_grad, weight, (((1,), (1,)), ((), ())), preferred_element_type=jnp.float32
    ).astype(jnp.bfloat16)
    grad_cols = lax.all_to_all(
        attn_grad[None, :, half:], "seq", split_axis=1, concat_axis=0, tiled=True
    ).reshape(rows, cols_each, heads_half, DH)
    col_grads = column_backward(
        col_q, col_k, col_v, col_out, grad_cols, col_scores, col_total, col_ok
    )
    col_grads_back = lax.all_to_all(
        jnp.stack([g.reshape(rows, cols_each, half) for g in col_grads]),
        "seq",
        split_axis=1,
        concat_axis=2,
        tiled=True,
    )

    row_grads = row_backward(
        row_q,
        row_k,
        row_v,
        row_out,
        attn_grad[:, :half].reshape(tokens, heads_half, DH),
        row_scores,
        row_total,
        row_ok,
    )

    layer_out = jnp.dot(attention, weight, preferred_element_type=jnp.float32).astype(
        jnp.bfloat16
    )

    grads = [
        jnp.concatenate([row_grads[i].reshape(tokens, half), col_grads_back[i, 0]], axis=1)[
            None, None
        ]
        for i in range(3)
    ]
    return (layer_out[None, None], grads[0], grads[1], grads[2], wo_grad)


def solution(mesh):
    in_specs = (
        P("dp", "seq", None, None),
        P("dp", "seq", None, None),
        P("dp", "seq", None, None),
        P("dp", "seq", None, None),
        P("dp", None),
        P(),
        P(),
    )
    out_specs = (
        P("dp", "seq", None, None),
        P("dp", "seq", None, None),
        P("dp", "seq", None, None),
        P("dp", "seq", None, None),
        P(("dp", "seq"), None),
    )
    return jax.shard_map(
        on_device, mesh=mesh, in_specs=in_specs, out_specs=out_specs, check_vma=False
    )
```

```python
import math

import jax
import jax.numpy as jnp
from jax import lax
from jax.sharding import PartitionSpec as P

DH = 128
COLS = 512
BLK = 128

masked_out = -1e30
scale = 1.0 / math.sqrt(DH)


def row_permit(row_mask):
    spread = jnp.repeat(jnp.repeat(row_mask, BLK, axis=0), BLK, axis=1)
    row_index = lax.broadcasted_iota(jnp.int32, (COLS, COLS), 0)
    col_index = lax.broadcasted_iota(jnp.int32, (COLS, COLS), 1)
    return (spread == 1) & (col_index <= row_index)


def softmax_parts(scores, allowed):
    highest = jnp.max(jnp.where(allowed, scores, masked_out), axis=-1, keepdims=True)
    attend = jnp.exp(jnp.where(allowed, scores - highest, masked_out))
    totals = jnp.sum(attend, axis=-1, keepdims=True)
    probs = (attend / totals).astype(jnp.bfloat16)
    return probs, highest + jnp.log(totals)


def row_forward(q, k, v, allowed):
    scores = jnp.einsum("ihd,jhd->hij", q, k, preferred_element_type=jnp.float32) * scale
    probs, log_total = softmax_parts(scores, allowed[None])
    out = jnp.einsum("hij,jhd->ihd", probs, v, preferred_element_type=jnp.float32)
    return out.astype(jnp.bfloat16), scores, log_total


def row_backward(q, k, v, out, grad, scores, log_total, allowed):
    grad_dot = jnp.einsum("ihd,ihd->hi", grad, out, preferred_element_type=jnp.float32)
    back = jnp.where(allowed[None], jnp.exp(scores - log_total), 0.0)
    value_grad = jnp.einsum(
        "hij,ihd->jhd", back.astype(jnp.bfloat16), grad, preferred_element_type=jnp.float32
    )
    prob_grad = jnp.einsum("ihd,jhd->hij", grad, v, preferred_element_type=jnp.float32)
    score_grad = (back * (prob_grad - grad_dot[..., None])).astype(jnp.bfloat16)
    query_grad = jnp.einsum("hij,jhd->ihd", score_grad, k, preferred_element_type=jnp.float32)
    key_grad = jnp.einsum("hij,ihd->jhd", score_grad, q, preferred_element_type=jnp.float32)
    return tuple(
        g.astype(jnp.bfloat16) for g in (query_grad * scale, key_grad * scale, value_grad)
    )


def column_forward(q, k, v, allowed):
    scores = jnp.einsum("rchd,schd->chrs", q, k, preferred_element_type=jnp.float32) * scale
    probs, log_total = softmax_parts(scores, allowed)
    out = jnp.einsum("chrs,schd->rchd", probs, v, preferred_element_type=jnp.float32)
    return out.astype(jnp.bfloat16), scores, log_total


def column_backward(q, k, v, out, grad, scores, log_total, allowed):
    grad_dot = jnp.einsum("rchd,rchd->chr", grad, out, preferred_element_type=jnp.float32)
    back = jnp.where(allowed, jnp.exp(scores - log_total), 0.0)
    value_grad = jnp.einsum(
        "chrs,rchd->schd", back.astype(jnp.bfloat16), grad, preferred_element_type=jnp.float32
    )
    prob_grad = jnp.einsum("rchd,schd->chrs", grad, v, preferred_element_type=jnp.float32)
    score_grad = (back * (prob_grad - grad_dot[..., None])).astype(jnp.bfloat16)
    query_grad = jnp.einsum("chrs,schd->rchd", score_grad, k, preferred_element_type=jnp.float32)
    key_grad = jnp.einsum("chrs,rchd->schd", score_grad, q, preferred_element_type=jnp.float32)
    return tuple(
        g.astype(jnp.bfloat16) for g in (query_grad * scale, key_grad * scale, value_grad)
    )


def on_device(queries, keys, values, out_grad, out_weight, row_mask, col_mask):
    tokens, features = queries.shape[2], queries.shape[3]
    half = features // 2
    heads_half = half // DH
    rows = lax.axis_size("seq")
    cols_each = tokens // rows
    weight = lax.all_gather(out_weight, "dp", axis=0, tiled=True)
    core = lax.axis_index("seq") % 2
    pairs = [(2 * m + j, 2 * m + 1 - j) for m in range(rows // 2) for j in range(2)]
    grad_mate = lax.ppermute(out_grad[0, 0], "seq", pairs)

    packed = jnp.stack([t[0, 0, :, half:] for t in (queries, keys, values)])
    shipped = lax.all_to_all(packed[None], "seq", split_axis=2, concat_axis=0, tiled=True)
    col_q, col_k, col_v = (
        shipped[:, i].reshape(rows, cols_each, heads_half, DH) for i in range(3)
    )
    col_ok = col_mask == 1
    col_out, col_scores, col_total = column_forward(col_q, col_k, col_v, col_ok)
    col_back = lax.all_to_all(
        col_out.reshape(rows, cols_each, half), "seq", split_axis=0, concat_axis=1, tiled=True
    )

    row_ok = row_permit(row_mask)
    split = lambda t: t[0, 0, :, :half].reshape(tokens, heads_half, DH)
    row_q, row_k, row_v = split(queries), split(keys), split(values)
    row_out, row_scores, row_total = row_forward(row_q, row_k, row_v, row_ok)

    flat_grad = out_grad[0, 0]
    attention = jnp.concatenate([row_out.reshape(tokens, half), col_back[0]], axis=1)

    dp_size = lax.axis_size("dp")
    block = features // (dp_size * rows)
    by_parity = attention.reshape(tokens, features // (2 * block), 2, block)
    own_rows = jnp.where(core == 0, by_parity[:, :, 0], by_parity[:, :, 1])
    mate_rows = lax.ppermute(
        jnp.where(core == 0, by_parity[:, :, 1], by_parity[:, :, 0]), "seq", pairs
    )
    pair_attn = jnp.concatenate([own_rows, mate_rows], axis=0).reshape(2 * tokens, features // 2)
    pair_grad = jnp.concatenate([flat_grad, grad_mate], axis=0)
    partial = lax.dot_general(
        pair_attn, pair_grad, (((0,), (0,)), ((), ())), preferred_element_type=jnp.float32
    ).reshape(dp_size, rows // 2, block, features)
    partial, weight = lax.optimization_barrier((partial, weight))
    over_dp = lax.all_to_all(partial, "dp", split_axis=0, concat_axis=0, tiled=True).sum(axis=0)
    parity_groups = [[2 * m + c for m in range(rows // 2)] for c in range(2)]
    over_z = lax.all_to_all(
        over_dp, "seq", split_axis=0, concat_axis=0, tiled=True, axis_index_groups=parity_groups
    ).sum(axis=0)
    wo_grad = over_z * (1.0 / math.sqrt(tokens * dp_size * rows))

    attn_grad = lax.dot_general(
        flat_grad, weight, (((1,), (1,)), ((), ())), preferred_element_type=jnp.float32
    ).astype(jnp.bfloat16)
    grad_cols = lax.all_to_all(
        attn_grad[None, :, half:], "seq", split_axis=1, concat_axis=0, tiled=True
    ).reshape(rows, cols_each, heads_half, DH)
    col_grads = column_backward(
        col_q, col_k, col_v, col_out, grad_cols, col_scores, col_total, col_ok
    )
    col_grads_back = lax.all_to_all(
        jnp.stack([g.reshape(rows, cols_each, half) for g in col_grads]),
        "seq",
        split_axis=1,
        concat_axis=2,
        tiled=True,
    )

    row_grads = row_backward(
        row_q,
        row_k,
        row_v,
        row_out,
        attn_grad[:, :half].reshape(tokens, heads_half, DH),
        row_scores,
        row_total,
        row_ok,
    )

    layer_out = jnp.dot(attention, weight, preferred_element_type=jnp.float32).astype(
        jnp.bfloat16
    )

    grads = [
        jnp.concatenate([row_grads[i].reshape(tokens, half), col_grads_back[i, 0]], axis=1)[
            None, None
        ]
        for i in range(3)
    ]
    return (layer_out[None, None], grads[0], grads[1], grads[2], wo_grad)


def solution(mesh):
    in_specs = (
        P("dp", "seq", None, None),
        P("dp", "seq", None, None),
        P("dp", "seq", None, None),
        P("dp", "seq", None, None),
        P("dp", None),
        P(),
        P(),
    )
    out_specs = (
        P("dp", "seq", None, None),
        P("dp", "seq", None, None),
        P("dp", "seq", None, None),
        P("dp", "seq", None, None),
        P(("dp", "seq"), None),
    )
    return jax.shard_map(
        on_device, mesh=mesh, in_specs=in_specs, out_specs=out_specs, check_vma=False
    )
```

```python
import math

import jax
import jax.numpy as jnp
from jax import lax
from jax.sharding import PartitionSpec as P

DH = 128
COLS = 512
BLK = 128

masked_out = -1e30
scale = 1.0 / math.sqrt(DH)


def row_permit(row_mask):
    spread = jnp.repeat(jnp.repeat(row_mask, BLK, axis=0), BLK, axis=1)
    row_index = lax.broadcasted_iota(jnp.int32, (COLS, COLS), 0)
    col_index = lax.broadcasted_iota(jnp.int32, (COLS, COLS), 1)
    return (spread == 1) & (col_index <= row_index)


def softmax_parts(scores, allowed):
    highest = jnp.max(jnp.where(allowed, scores, masked_out), axis=-1, keepdims=True)
    attend = jnp.exp(jnp.where(allowed, scores - highest, masked_out))
    totals = jnp.sum(attend, axis=-1, keepdims=True)
    probs = (attend / totals).astype(jnp.bfloat16)
    return probs, highest + jnp.log(totals)


def row_forward(q, k, v, allowed):
    scores = jnp.einsum("ihd,jhd->hij", q, k, preferred_element_type=jnp.float32) * scale
    probs, log_total = softmax_parts(scores, allowed[None])
    out = jnp.einsum("hij,jhd->ihd", probs, v, preferred_element_type=jnp.float32)
    return out.astype(jnp.bfloat16), scores, log_total


def row_backward(q, k, v, out, grad, scores, log_total, allowed):
    grad_dot = jnp.einsum("ihd,ihd->hi", grad, out, preferred_element_type=jnp.float32)
    back = jnp.where(allowed[None], jnp.exp(scores - log_total), 0.0)
    value_grad = jnp.einsum(
        "hij,ihd->jhd", back.astype(jnp.bfloat16), grad, preferred_element_type=jnp.float32
    )
    prob_grad = jnp.einsum("ihd,jhd->hij", grad, v, preferred_element_type=jnp.float32)
    score_grad = (back * (prob_grad - grad_dot[..., None])).astype(jnp.bfloat16)
    query_grad = jnp.einsum("hij,jhd->ihd", score_grad, k, preferred_element_type=jnp.float32)
    key_grad = jnp.einsum("hij,ihd->jhd", score_grad, q, preferred_element_type=jnp.float32)
    return tuple(
        g.astype(jnp.bfloat16) for g in (query_grad * scale, key_grad * scale, value_grad)
    )


def column_forward(q, k, v, allowed):
    scores = jnp.einsum("rchd,schd->chrs", q, k, preferred_element_type=jnp.float32) * scale
    probs, log_total = softmax_parts(scores, allowed)
    out = jnp.einsum("chrs,schd->rchd", probs, v, preferred_element_type=jnp.float32)
    return out.astype(jnp.bfloat16), scores, log_total


def column_backward(q, k, v, out, grad, scores, log_total, allowed):
    grad_dot = jnp.einsum("rchd,rchd->chr", grad, out, preferred_element_type=jnp.float32)
    back = jnp.where(allowed, jnp.exp(scores - log_total), 0.0)
    value_grad = jnp.einsum(
        "chrs,rchd->schd", back.astype(jnp.bfloat16), grad, preferred_element_type=jnp.float32
    )
    prob_grad = jnp.einsum("rchd,schd->chrs", grad, v, preferred_element_type=jnp.float32)
    score_grad = (back * (prob_grad - grad_dot[..., None])).astype(jnp.bfloat16)
    query_grad = jnp.einsum("chrs,schd->rchd", score_grad, k, preferred_element_type=jnp.float32)
    key_grad = jnp.einsum("chrs,rchd->schd", score_grad, q, preferred_element_type=jnp.float32)
    return tuple(
        g.astype(jnp.bfloat16) for g in (query_grad * scale, key_grad * scale, value_grad)
    )


def on_device(queries, keys, values, out_grad, out_weight, row_mask, col_mask):
    tokens, features = queries.shape[2], queries.shape[3]
    half = features // 2
    heads_half = half // DH
    rows = lax.axis_size("seq")
    cols_each = tokens // rows

    dp_size = lax.axis_size("dp")
    dp_index = lax.axis_index("dp")
    shifted = [out_weight] + [
        lax.ppermute(out_weight, "dp", [(i, (i + k) % dp_size) for i in range(dp_size)])
        for k in range(1, dp_size)
    ]
    weight = jnp.take(
        jnp.stack(shifted), (dp_index - jnp.arange(dp_size)) % dp_size, axis=0
    ).reshape(features, features)

    packed = jnp.stack([t[0, 0, :, half:] for t in (queries, keys, values)])
    shipped = lax.all_to_all(packed[None], "seq", split_axis=2, concat_axis=0, tiled=True)
    col_q, col_k, col_v = (
        shipped[:, i].reshape(rows, cols_each, heads_half, DH) for i in range(3)
    )
    col_ok = col_mask == 1
    col_out, col_scores, col_total = column_forward(col_q, col_k, col_v, col_ok)
    col_back = lax.all_to_all(
        col_out.reshape(rows, cols_each, half), "seq", split_axis=0, concat_axis=1, tiled=True
    )

    row_ok = row_permit(row_mask)
    split = lambda t: t[0, 0, :, :half].reshape(tokens, heads_half, DH)
    row_q, row_k, row_v = split(queries), split(keys), split(values)
    row_out, row_scores, row_total = row_forward(row_q, row_k, row_v, row_ok)

    flat_grad = out_grad[0, 0]
    half_dp = dp_size // 2
    order = [
        member
        for d in range(half_dp)
        for s in range(rows)
        for member in (d * rows + s, (d + half_dp) * rows + s)
    ]
    row_attn = row_out.reshape(tokens, half)
    row_partial = lax.dot_general(
        row_attn, flat_grad, (((0,), (0,)), ((), ())), preferred_element_type=jnp.float32
    )
    row_piece = lax.psum_scatter(
        row_partial, ("dp", "seq"), scatter_dimension=0, tiled=True, axis_index_groups=[order]
    )
    attention = jnp.concatenate([row_attn, col_back[0]], axis=1)
    col_partial = lax.dot_general(
        col_back[0], flat_grad, (((0,), (0,)), ((), ())), preferred_element_type=jnp.float32
    )
    col_partial, weight = lax.optimization_barrier((col_partial, weight))
    col_piece = lax.psum_scatter(
        col_partial, ("dp", "seq"), scatter_dimension=0, tiled=True, axis_index_groups=[order]
    )
    is_x = dp_index < half_dp
    swap = [(d, d + half_dp) for d in range(half_dp)] + [(d + half_dp, d) for d in range(half_dp)]
    received = lax.ppermute(jnp.where(is_x, col_piece, row_piece), "dp", swap)
    wo_grad = jnp.concatenate(
        [jnp.where(is_x, row_piece, received), jnp.where(is_x, received, col_piece)], axis=0
    ) * (1.0 / math.sqrt(tokens * dp_size * rows))

    attn_grad = lax.dot_general(
        flat_grad, weight, (((1,), (1,)), ((), ())), preferred_element_type=jnp.float32
    ).astype(jnp.bfloat16)
    grad_cols = lax.all_to_all(
        attn_grad[None, :, half:], "seq", split_axis=1, concat_axis=0, tiled=True
    ).reshape(rows, cols_each, heads_half, DH)
    col_grads = column_backward(
        col_q, col_k, col_v, col_out, grad_cols, col_scores, col_total, col_ok
    )
    col_grads_back = lax.all_to_all(
        jnp.stack([g.reshape(rows, cols_each, half) for g in col_grads]),
        "seq",
        split_axis=1,
        concat_axis=2,
        tiled=True,
    )

    row_grads = row_backward(
        row_q,
        row_k,
        row_v,
        row_out,
        attn_grad[:, :half].reshape(tokens, heads_half, DH),
        row_scores,
        row_total,
        row_ok,
    )

    layer_out = jnp.dot(attention, weight, preferred_element_type=jnp.float32).astype(
        jnp.bfloat16
    )

    grads = [
        jnp.concatenate([row_grads[i].reshape(tokens, half), col_grads_back[i, 0]], axis=1)[
            None, None
        ]
        for i in range(3)
    ]
    return (layer_out[None, None], grads[0], grads[1], grads[2], wo_grad)


def solution(mesh):
    in_specs = (
        P("dp", "seq", None, None),
        P("dp", "seq", None, None),
        P("dp", "seq", None, None),
        P("dp", "seq", None, None),
        P("dp", None),
        P(),
        P(),
    )
    out_specs = (
        P("dp", "seq", None, None),
        P("dp", "seq", None, None),
        P("dp", "seq", None, None),
        P("dp", "seq", None, None),
        P(("dp", "seq"), None),
    )
    return jax.shard_map(
        on_device, mesh=mesh, in_specs=in_specs, out_specs=out_specs, check_vma=False
    )
```

```python
import math

import jax
import jax.numpy as jnp
from jax import lax
from jax.sharding import PartitionSpec as P

DH = 128
COLS = 512
BLK = 128

masked_out = -1e30
scale = 1.0 / math.sqrt(DH)


def row_permit(row_mask):
    spread = jnp.repeat(jnp.repeat(row_mask, BLK, axis=0), BLK, axis=1)
    row_index = lax.broadcasted_iota(jnp.int32, (COLS, COLS), 0)
    col_index = lax.broadcasted_iota(jnp.int32, (COLS, COLS), 1)
    return (spread == 1) & (col_index <= row_index)


def softmax_parts(scores, allowed):
    highest = jnp.max(jnp.where(allowed, scores, masked_out), axis=-1, keepdims=True)
    attend = jnp.exp(jnp.where(allowed, scores - highest, masked_out))
    totals = jnp.sum(attend, axis=-1, keepdims=True)
    probs = (attend / totals).astype(jnp.bfloat16)
    return probs, highest + jnp.log(totals)


def row_forward(q, k, v, allowed):
    scores = jnp.einsum("ihd,jhd->hij", q, k, preferred_element_type=jnp.float32) * scale
    probs, log_total = softmax_parts(scores, allowed[None])
    out = jnp.einsum("hij,jhd->ihd", probs, v, preferred_element_type=jnp.float32)
    return out.astype(jnp.bfloat16), scores, log_total


def row_backward(q, k, v, out, grad, scores, log_total, allowed):
    grad_dot = jnp.einsum("ihd,ihd->hi", grad, out, preferred_element_type=jnp.float32)
    back = jnp.where(allowed[None], jnp.exp(scores - log_total), 0.0)
    value_grad = jnp.einsum(
        "hij,ihd->jhd", back.astype(jnp.bfloat16), grad, preferred_element_type=jnp.float32
    )
    prob_grad = jnp.einsum("ihd,jhd->hij", grad, v, preferred_element_type=jnp.float32)
    score_grad = (back * (prob_grad - grad_dot[..., None])).astype(jnp.bfloat16)
    query_grad = jnp.einsum("hij,jhd->ihd", score_grad, k, preferred_element_type=jnp.float32)
    key_grad = jnp.einsum("hij,ihd->jhd", score_grad, q, preferred_element_type=jnp.float32)
    return tuple(
        g.astype(jnp.bfloat16) for g in (query_grad * scale, key_grad * scale, value_grad)
    )


def column_forward(q, k, v, allowed):
    scores = jnp.einsum("rchd,schd->chrs", q, k, preferred_element_type=jnp.float32) * scale
    probs, log_total = softmax_parts(scores, allowed)
    out = jnp.einsum("chrs,schd->rchd", probs, v, preferred_element_type=jnp.float32)
    return out.astype(jnp.bfloat16), scores, log_total


def column_backward(q, k, v, out, grad, scores, log_total, allowed):
    grad_dot = jnp.einsum("rchd,rchd->chr", grad, out, preferred_element_type=jnp.float32)
    back = jnp.where(allowed, jnp.exp(scores - log_total), 0.0)
    value_grad = jnp.einsum(
        "chrs,rchd->schd", back.astype(jnp.bfloat16), grad, preferred_element_type=jnp.float32
    )
    prob_grad = jnp.einsum("rchd,schd->chrs", grad, v, preferred_element_type=jnp.float32)
    score_grad = (back * (prob_grad - grad_dot[..., None])).astype(jnp.bfloat16)
    query_grad = jnp.einsum("chrs,schd->rchd", score_grad, k, preferred_element_type=jnp.float32)
    key_grad = jnp.einsum("chrs,rchd->schd", score_grad, q, preferred_element_type=jnp.float32)
    return tuple(
        g.astype(jnp.bfloat16) for g in (query_grad * scale, key_grad * scale, value_grad)
    )


def on_device(queries, keys, values, out_grad, out_weight, row_mask, col_mask):
    tokens, features = queries.shape[2], queries.shape[3]
    half = features // 2
    heads_half = half // DH
    rows = lax.axis_size("seq")
    cols_each = tokens // rows

    weight = lax.all_gather(out_weight, "dp", axis=0, tiled=True)

    packed = jnp.stack([t[0, 0, :, half:] for t in (queries, keys, values)])
    shipped = lax.all_to_all(packed[None], "seq", split_axis=2, concat_axis=0, tiled=True)
    col_q, col_k, col_v = (
        shipped[:, i].reshape(rows, cols_each, heads_half, DH) for i in range(3)
    )
    col_ok = col_mask == 1
    col_out, col_scores, col_total = column_forward(col_q, col_k, col_v, col_ok)
    col_back = lax.all_to_all(
        col_out.reshape(rows, cols_each, half), "seq", split_axis=0, concat_axis=1, tiled=True
    )

    row_ok = row_permit(row_mask)
    split = lambda t: t[0, 0, :, :half].reshape(tokens, heads_half, DH)
    row_q, row_k, row_v = split(queries), split(keys), split(values)
    row_out, row_scores, row_total = row_forward(row_q, row_k, row_v, row_ok)

    flat_grad = out_grad[0, 0]
    attention = jnp.concatenate([row_out.reshape(tokens, half), col_back[0]], axis=1)
    partial = lax.dot_general(
        attention, flat_grad, (((0,), (0,)), ((), ())), preferred_element_type=jnp.float32
    )
    partial, weight = lax.optimization_barrier((partial, weight))
    devices_all = lax.axis_size(("dp", "seq"))
    wo_grad = lax.psum_scatter(
        partial.astype(jnp.bfloat16), ("dp", "seq"), scatter_dimension=0, tiled=True
    ).astype(jnp.float32) * (1.0 / math.sqrt(tokens * devices_all))

    attn_grad = lax.dot_general(
        flat_grad, weight, (((1,), (1,)), ((), ())), preferred_element_type=jnp.float32
    ).astype(jnp.bfloat16)
    grad_cols = lax.all_to_all(
        attn_grad[None, :, half:], "seq", split_axis=1, concat_axis=0, tiled=True
    ).reshape(rows, cols_each, heads_half, DH)
    col_grads = column_backward(
        col_q, col_k, col_v, col_out, grad_cols, col_scores, col_total, col_ok
    )
    col_grads_back = lax.all_to_all(
        jnp.stack([g.reshape(rows, cols_each, half) for g in col_grads]),
        "seq",
        split_axis=1,
        concat_axis=2,
        tiled=True,
    )

    row_grads = row_backward(
        row_q,
        row_k,
        row_v,
        row_out,
        attn_grad[:, :half].reshape(tokens, heads_half, DH),
        row_scores,
        row_total,
        row_ok,
    )

    layer_out = jnp.dot(attention, weight, preferred_element_type=jnp.float32).astype(
        jnp.bfloat16
    )

    grads = [
        jnp.concatenate([row_grads[i].reshape(tokens, half), col_grads_back[i, 0]], axis=1)[
            None, None
        ]
        for i in range(3)
    ]
    return (layer_out[None, None], grads[0], grads[1], grads[2], wo_grad)


def solution(mesh):
    in_specs = (
        P("dp", "seq", None, None),
        P("dp", "seq", None, None),
        P("dp", "seq", None, None),
        P("dp", "seq", None, None),
        P("dp", None),
        P(),
        P(),
    )
    out_specs = (
        P("dp", "seq", None, None),
        P("dp", "seq", None, None),
        P("dp", "seq", None, None),
        P("dp", "seq", None, None),
        P(("dp", "seq"), None),
    )
    return jax.shard_map(
        on_device, mesh=mesh, in_specs=in_specs, out_specs=out_specs, check_vma=False
    )
```

```python
import math

import jax
import jax.numpy as jnp
from jax import lax
from jax.sharding import PartitionSpec as P

DH = 128
COLS = 512
BLK = 128

masked_out = -1e30
scale = 1.0 / math.sqrt(DH)


def row_permit(row_mask):
    spread = jnp.repeat(jnp.repeat(row_mask, BLK, axis=0), BLK, axis=1)
    row_index = lax.broadcasted_iota(jnp.int32, (COLS, COLS), 0)
    col_index = lax.broadcasted_iota(jnp.int32, (COLS, COLS), 1)
    return (spread == 1) & (col_index <= row_index)


def softmax_parts(scores, allowed):
    highest = jnp.max(jnp.where(allowed, scores, masked_out), axis=-1, keepdims=True)
    attend = jnp.exp(jnp.where(allowed, scores - highest, masked_out))
    totals = jnp.sum(attend, axis=-1, keepdims=True)
    probs = (attend / totals).astype(jnp.bfloat16)
    return probs, highest + jnp.log(totals)


def row_forward(q, k, v, allowed):
    scores = jnp.einsum("ihd,jhd->hij", q, k, preferred_element_type=jnp.float32) * scale
    probs, log_total = softmax_parts(scores, allowed[None])
    out = jnp.einsum("hij,jhd->ihd", probs, v, preferred_element_type=jnp.float32)
    return out.astype(jnp.bfloat16), scores, log_total


def row_backward(q, k, v, out, grad, scores, log_total, allowed):
    grad_dot = jnp.einsum("ihd,ihd->hi", grad, out, preferred_element_type=jnp.float32)
    back = jnp.where(allowed[None], jnp.exp(scores - log_total), 0.0)
    value_grad = jnp.einsum(
        "hij,ihd->jhd", back.astype(jnp.bfloat16), grad, preferred_element_type=jnp.float32
    )
    prob_grad = jnp.einsum("ihd,jhd->hij", grad, v, preferred_element_type=jnp.float32)
    score_grad = (back * (prob_grad - grad_dot[..., None])).astype(jnp.bfloat16)
    query_grad = jnp.einsum("hij,jhd->ihd", score_grad, k, preferred_element_type=jnp.float32)
    key_grad = jnp.einsum("hij,ihd->jhd", score_grad, q, preferred_element_type=jnp.float32)
    return tuple(
        g.astype(jnp.bfloat16) for g in (query_grad * scale, key_grad * scale, value_grad)
    )


def column_forward(q, k, v, allowed):
    scores = jnp.einsum("rchd,schd->chrs", q, k, preferred_element_type=jnp.float32) * scale
    probs, log_total = softmax_parts(scores, allowed)
    out = jnp.einsum("chrs,schd->rchd", probs, v, preferred_element_type=jnp.float32)
    return out.astype(jnp.bfloat16), scores, log_total


def column_backward(q, k, v, out, grad, scores, log_total, allowed):
    grad_dot = jnp.einsum("rchd,rchd->chr", grad, out, preferred_element_type=jnp.float32)
    back = jnp.where(allowed, jnp.exp(scores - log_total), 0.0)
    value_grad = jnp.einsum(
        "chrs,rchd->schd", back.astype(jnp.bfloat16), grad, preferred_element_type=jnp.float32
    )
    prob_grad = jnp.einsum("rchd,schd->chrs", grad, v, preferred_element_type=jnp.float32)
    score_grad = (back * (prob_grad - grad_dot[..., None])).astype(jnp.bfloat16)
    query_grad = jnp.einsum("chrs,schd->rchd", score_grad, k, preferred_element_type=jnp.float32)
    key_grad = jnp.einsum("chrs,rchd->schd", score_grad, q, preferred_element_type=jnp.float32)
    return tuple(
        g.astype(jnp.bfloat16) for g in (query_grad * scale, key_grad * scale, value_grad)
    )


def on_device(queries, keys, values, out_grad, out_weight, row_mask, col_mask):
    tokens, features = queries.shape[2], queries.shape[3]
    half = features // 2
    heads_half = half // DH
    rows = lax.axis_size("seq")
    cols_each = tokens // rows

    weight = lax.all_gather(out_weight, "dp", axis=0, tiled=True)

    packed = jnp.stack([t[0, 0, :, half:] for t in (queries, keys, values)])
    shipped = lax.all_to_all(packed[None], "seq", split_axis=2, concat_axis=0, tiled=True)
    col_q, col_k, col_v = (
        shipped[:, i].reshape(rows, cols_each, heads_half, DH) for i in range(3)
    )
    col_ok = col_mask == 1
    col_out, col_scores, col_total = column_forward(col_q, col_k, col_v, col_ok)
    col_back = lax.all_to_all(
        col_out.reshape(rows, cols_each, half), "seq", split_axis=0, concat_axis=1, tiled=True
    )

    row_ok = row_permit(row_mask)
    split = lambda t: t[0, 0, :, :half].reshape(tokens, heads_half, DH)
    row_q, row_k, row_v = split(queries), split(keys), split(values)
    row_out, row_scores, row_total = row_forward(row_q, row_k, row_v, row_ok)

    flat_grad = out_grad[0, 0]
    attention = jnp.concatenate([row_out.reshape(tokens, half), col_back[0]], axis=1)
    partial = lax.dot_general(
        attention, flat_grad, (((0,), (0,)), ((), ())), preferred_element_type=jnp.float32
    )

    attn_grad = lax.dot_general(
        flat_grad, weight, (((1,), (1,)), ((), ())), preferred_element_type=jnp.float32
    ).astype(jnp.bfloat16)
    partial, grad_col_part = lax.optimization_barrier((partial, attn_grad[None, :, half:]))
    devices_all = lax.axis_size(("dp", "seq"))
    wo_grad = lax.psum_scatter(
        partial.astype(jnp.bfloat16), ("dp", "seq"), scatter_dimension=0, tiled=True
    ).astype(jnp.float32) * (1.0 / math.sqrt(tokens * devices_all))
    grad_cols = lax.all_to_all(
        grad_col_part, "seq", split_axis=1, concat_axis=0, tiled=True
    ).reshape(rows, cols_each, heads_half, DH)
    col_grads = column_backward(
        col_q, col_k, col_v, col_out, grad_cols, col_scores, col_total, col_ok
    )
    col_grads_back = lax.all_to_all(
        jnp.stack([g.reshape(rows, cols_each, half) for g in col_grads]),
        "seq",
        split_axis=1,
        concat_axis=2,
        tiled=True,
    )

    row_grads = row_backward(
        row_q,
        row_k,
        row_v,
        row_out,
        attn_grad[:, :half].reshape(tokens, heads_half, DH),
        row_scores,
        row_total,
        row_ok,
    )

    layer_out = jnp.dot(attention, weight, preferred_element_type=jnp.float32).astype(
        jnp.bfloat16
    )

    grads = [
        jnp.concatenate([row_grads[i].reshape(tokens, half), col_grads_back[i, 0]], axis=1)[
            None, None
        ]
        for i in range(3)
    ]
    return (layer_out[None, None], grads[0], grads[1], grads[2], wo_grad)


def solution(mesh):
    in_specs = (
        P("dp", "seq", None, None),
        P("dp", "seq", None, None),
        P("dp", "seq", None, None),
        P("dp", "seq", None, None),
        P("dp", None),
        P(),
        P(),
    )
    out_specs = (
        P("dp", "seq", None, None),
        P("dp", "seq", None, None),
        P("dp", "seq", None, None),
        P("dp", "seq", None, None),
        P(("dp", "seq"), None),
    )
    return jax.shard_map(
        on_device, mesh=mesh, in_specs=in_specs, out_specs=out_specs, check_vma=False
    )
```

```python
import math

import jax
import jax.numpy as jnp
from jax import lax
from jax.sharding import PartitionSpec as P

DH = 128
COLS = 512
BLK = 128

masked_out = -1e30
scale = 1.0 / math.sqrt(DH)


def row_permit(row_mask):
    spread = jnp.repeat(jnp.repeat(row_mask, BLK, axis=0), BLK, axis=1)
    row_index = lax.broadcasted_iota(jnp.int32, (COLS, COLS), 0)
    col_index = lax.broadcasted_iota(jnp.int32, (COLS, COLS), 1)
    return (spread == 1) & (col_index <= row_index)


def softmax_parts(scores, allowed):
    highest = jnp.max(jnp.where(allowed, scores, masked_out), axis=-1, keepdims=True)
    attend = jnp.exp(jnp.where(allowed, scores - highest, masked_out))
    totals = jnp.sum(attend, axis=-1, keepdims=True)
    probs = (attend / totals).astype(jnp.bfloat16)
    return probs, highest + jnp.log(totals)


def row_forward(q, k, v, allowed):
    scores = jnp.einsum("ihd,jhd->hij", q, k, preferred_element_type=jnp.float32) * scale
    probs, log_total = softmax_parts(scores, allowed[None])
    out = jnp.einsum("hij,jhd->ihd", probs, v, preferred_element_type=jnp.float32)
    return out.astype(jnp.bfloat16), scores, log_total


def row_backward(q, k, v, out, grad, scores, log_total, allowed):
    grad_dot = jnp.einsum("ihd,ihd->hi", grad, out, preferred_element_type=jnp.float32)
    back = jnp.where(allowed[None], jnp.exp(scores - log_total), 0.0)
    value_grad = jnp.einsum(
        "hij,ihd->jhd", back.astype(jnp.bfloat16), grad, preferred_element_type=jnp.float32
    )
    prob_grad = jnp.einsum("ihd,jhd->hij", grad, v, preferred_element_type=jnp.float32)
    score_grad = (back * (prob_grad - grad_dot[..., None])).astype(jnp.bfloat16)
    query_grad = jnp.einsum("hij,jhd->ihd", score_grad, k, preferred_element_type=jnp.float32)
    key_grad = jnp.einsum("hij,ihd->jhd", score_grad, q, preferred_element_type=jnp.float32)
    return tuple(
        g.astype(jnp.bfloat16) for g in (query_grad * scale, key_grad * scale, value_grad)
    )


def column_forward(q, k, v, allowed):
    scores = jnp.einsum("rchd,schd->chrs", q, k, preferred_element_type=jnp.float32) * scale
    probs, log_total = softmax_parts(scores, allowed)
    out = jnp.einsum("chrs,schd->rchd", probs, v, preferred_element_type=jnp.float32)
    return out.astype(jnp.bfloat16), scores, log_total


def column_backward(q, k, v, out, grad, scores, log_total, allowed):
    grad_dot = jnp.einsum("rchd,rchd->chr", grad, out, preferred_element_type=jnp.float32)
    back = jnp.where(allowed, jnp.exp(scores - log_total), 0.0)
    value_grad = jnp.einsum(
        "chrs,rchd->schd", back.astype(jnp.bfloat16), grad, preferred_element_type=jnp.float32
    )
    prob_grad = jnp.einsum("rchd,schd->chrs", grad, v, preferred_element_type=jnp.float32)
    score_grad = (back * (prob_grad - grad_dot[..., None])).astype(jnp.bfloat16)
    query_grad = jnp.einsum("chrs,schd->rchd", score_grad, k, preferred_element_type=jnp.float32)
    key_grad = jnp.einsum("chrs,rchd->schd", score_grad, q, preferred_element_type=jnp.float32)
    return tuple(
        g.astype(jnp.bfloat16) for g in (query_grad * scale, key_grad * scale, value_grad)
    )


def on_device(queries, keys, values, out_grad, out_weight, row_mask, col_mask):
    tokens, features = queries.shape[2], queries.shape[3]
    half = features // 2
    heads_half = half // DH
    rows = lax.axis_size("seq")
    cols_each = tokens // rows

    weight = lax.all_gather(out_weight, "dp", axis=0, tiled=True)

    chunks = 2
    piece = cols_each // chunks

    def chunked(t):
        return t.reshape(rows, chunks, piece, half).transpose(1, 0, 2, 3)

    packed = jnp.stack([chunked(t[0, 0, :, half:]) for t in (queries, keys, values)], axis=1)
    col_ok = col_mask == 1
    col_state = []
    col_back = []
    for j in range(chunks):
        shipped = lax.all_to_all(packed[j], "seq", split_axis=1, concat_axis=1, tiled=True)
        col_q, col_k, col_v = (
            shipped[i].reshape(rows, piece, heads_half, DH) for i in range(3)
        )
        col_out, col_scores, col_total = column_forward(col_q, col_k, col_v, col_ok)
        col_state.append((col_q, col_k, col_v, col_out, col_scores, col_total))
        col_back.append(
            lax.all_to_all(
                col_out.reshape(rows, piece, half), "seq", split_axis=0, concat_axis=0, tiled=True
            )
        )
    col_attn = jnp.stack(col_back, axis=1).reshape(tokens, half)

    row_ok = row_permit(row_mask)
    split = lambda t: t[0, 0, :, :half].reshape(tokens, heads_half, DH)
    row_q, row_k, row_v = split(queries), split(keys), split(values)
    row_out, row_scores, row_total = row_forward(row_q, row_k, row_v, row_ok)
    row_attn = row_out.reshape(tokens, half)

    flat_grad = out_grad[0, 0]
    attention = jnp.concatenate([row_attn, col_attn], axis=1)
    contract = (((0,), (0,)), ((), ()))
    row_partial = lax.dot_general(row_attn, flat_grad, contract, preferred_element_type=jnp.float32)
    col_partial = lax.dot_general(col_attn, flat_grad, contract, preferred_element_type=jnp.float32)
    partial = jnp.concatenate([row_partial, col_partial], axis=0)

    attn_grad = lax.dot_general(
        flat_grad, weight, (((1,), (1,)), ((), ())), preferred_element_type=jnp.float32
    ).astype(jnp.bfloat16)
    partial, grad_col_part = lax.optimization_barrier((partial, chunked(attn_grad[:, half:])))
    devices_all = lax.axis_size(("dp", "seq"))
    wo_grad = lax.psum_scatter(
        partial.astype(jnp.bfloat16), ("dp", "seq"), scatter_dimension=0, tiled=True
    ).astype(jnp.float32) * (1.0 / math.sqrt(tokens * devices_all))

    col_grads_back = []
    for j in range(chunks):
        grad_cols = lax.all_to_all(
            grad_col_part[j], "seq", split_axis=0, concat_axis=0, tiled=True
        ).reshape(rows, piece, heads_half, DH)
        col_q, col_k, col_v, col_out, col_scores, col_total = col_state[j]
        col_grads = column_backward(
            col_q, col_k, col_v, col_out, grad_cols, col_scores, col_total, col_ok
        )
        col_grads_back.append(
            lax.all_to_all(
                jnp.stack([g.reshape(rows, piece, half) for g in col_grads]),
                "seq",
                split_axis=1,
                concat_axis=1,
                tiled=True,
            )
        )
    col_grads_whole = jnp.stack(col_grads_back, axis=2).reshape(3, tokens, half)

    row_grads = row_backward(
        row_q,
        row_k,
        row_v,
        row_out,
        attn_grad[:, :half].reshape(tokens, heads_half, DH),
        row_scores,
        row_total,
        row_ok,
    )

    layer_out = jnp.dot(attention, weight, preferred_element_type=jnp.float32).astype(
        jnp.bfloat16
    )

    grads = [
        jnp.concatenate([row_grads[i].reshape(tokens, half), col_grads_whole[i]], axis=1)[
            None, None
        ]
        for i in range(3)
    ]
    return (layer_out[None, None], grads[0], grads[1], grads[2], wo_grad)


def solution(mesh):
    in_specs = (
        P("dp", "seq", None, None),
        P("dp", "seq", None, None),
        P("dp", "seq", None, None),
        P("dp", "seq", None, None),
        P("dp", None),
        P(),
        P(),
    )
    out_specs = (
        P("dp", "seq", None, None),
        P("dp", "seq", None, None),
        P("dp", "seq", None, None),
        P("dp", "seq", None, None),
        P(("dp", "seq"), None),
    )
    return jax.shard_map(
        on_device, mesh=mesh, in_specs=in_specs, out_specs=out_specs, check_vma=False
    )
```

```python
import math

import jax
import jax.numpy as jnp
from jax import lax
from jax.sharding import PartitionSpec as P

DH = 128
COLS = 512
BLK = 128

masked_out = -1e30
scale = 1.0 / math.sqrt(DH)


def row_permit(row_mask):
    spread = jnp.repeat(jnp.repeat(row_mask, BLK, axis=0), BLK, axis=1)
    row_index = lax.broadcasted_iota(jnp.int32, (COLS, COLS), 0)
    col_index = lax.broadcasted_iota(jnp.int32, (COLS, COLS), 1)
    return (spread == 1) & (col_index <= row_index)


def softmax_parts(scores, allowed):
    highest = jnp.max(jnp.where(allowed, scores, masked_out), axis=-1, keepdims=True)
    attend = jnp.exp(jnp.where(allowed, scores - highest, masked_out))
    totals = jnp.sum(attend, axis=-1, keepdims=True)
    probs = (attend / totals).astype(jnp.bfloat16)
    return probs, highest + jnp.log(totals)


def row_forward(q, k, v, allowed):
    scores = jnp.einsum("ihd,jhd->hij", q, k, preferred_element_type=jnp.float32) * scale
    probs, log_total = softmax_parts(scores, allowed[None])
    out = jnp.einsum("hij,jhd->ihd", probs, v, preferred_element_type=jnp.float32)
    return out.astype(jnp.bfloat16), scores, log_total


def row_backward(q, k, v, out, grad, scores, log_total, allowed):
    grad_dot = jnp.einsum("ihd,ihd->hi", grad, out, preferred_element_type=jnp.float32)
    back = jnp.where(allowed[None], jnp.exp(scores - log_total), 0.0)
    value_grad = jnp.einsum(
        "hij,ihd->jhd", back.astype(jnp.bfloat16), grad, preferred_element_type=jnp.float32
    )
    prob_grad = jnp.einsum("ihd,jhd->hij", grad, v, preferred_element_type=jnp.float32)
    score_grad = (back * (prob_grad - grad_dot[..., None])).astype(jnp.bfloat16)
    query_grad = jnp.einsum("hij,jhd->ihd", score_grad, k, preferred_element_type=jnp.float32)
    key_grad = jnp.einsum("hij,ihd->jhd", score_grad, q, preferred_element_type=jnp.float32)
    return tuple(
        g.astype(jnp.bfloat16) for g in (query_grad * scale, key_grad * scale, value_grad)
    )


def column_forward(q, k, v, allowed):
    scores = jnp.einsum("rchd,schd->chrs", q, k, preferred_element_type=jnp.float32) * scale
    probs, log_total = softmax_parts(scores, allowed)
    out = jnp.einsum("chrs,schd->rchd", probs, v, preferred_element_type=jnp.float32)
    return out.astype(jnp.bfloat16), scores, log_total


def column_backward(q, k, v, out, grad, scores, log_total, allowed):
    grad_dot = jnp.einsum("rchd,rchd->chr", grad, out, preferred_element_type=jnp.float32)
    back = jnp.where(allowed, jnp.exp(scores - log_total), 0.0)
    value_grad = jnp.einsum(
        "chrs,rchd->schd", back.astype(jnp.bfloat16), grad, preferred_element_type=jnp.float32
    )
    prob_grad = jnp.einsum("rchd,schd->chrs", grad, v, preferred_element_type=jnp.float32)
    score_grad = (back * (prob_grad - grad_dot[..., None])).astype(jnp.bfloat16)
    query_grad = jnp.einsum("chrs,schd->rchd", score_grad, k, preferred_element_type=jnp.float32)
    key_grad = jnp.einsum("chrs,rchd->schd", score_grad, q, preferred_element_type=jnp.float32)
    return tuple(
        g.astype(jnp.bfloat16) for g in (query_grad * scale, key_grad * scale, value_grad)
    )


def on_device(queries, keys, values, out_grad, out_weight, row_mask, col_mask):
    tokens, features = queries.shape[2], queries.shape[3]
    half = features // 2
    heads_half = half // DH
    rows = lax.axis_size("seq")
    cols_each = tokens // rows

    weight = lax.all_gather(out_weight, "dp", axis=0, tiled=True)

    chunks = 2
    piece = cols_each // chunks

    def chunked(t):
        return t.reshape(rows, chunks, piece, half).transpose(1, 0, 2, 3)

    packed = jnp.stack([chunked(t[0, 0, :, half:]) for t in (queries, keys, values)], axis=1)
    col_ok = col_mask == 1
    col_state = []
    col_back = []
    for j in range(chunks):
        shipped = lax.all_to_all(packed[j], "seq", split_axis=1, concat_axis=1, tiled=True)
        col_q, col_k, col_v = (
            shipped[i].reshape(rows, piece, heads_half, DH) for i in range(3)
        )
        col_out, col_scores, col_total = column_forward(col_q, col_k, col_v, col_ok)
        col_state.append((col_q, col_k, col_v, col_out, col_scores, col_total))
        col_back.append(
            lax.all_to_all(
                col_out.reshape(rows, piece, half), "seq", split_axis=0, concat_axis=0, tiled=True
            )
        )
    col_attn = jnp.stack(col_back, axis=1).reshape(tokens, half)

    row_ok = row_permit(row_mask)
    split = lambda t: t[0, 0, :, :half].reshape(tokens, heads_half, DH)
    row_q, row_k, row_v = split(queries), split(keys), split(values)
    row_out, row_scores, row_total = row_forward(row_q, row_k, row_v, row_ok)
    row_attn = row_out.reshape(tokens, half)

    flat_grad = out_grad[0, 0]
    attention = jnp.concatenate([row_attn, col_attn], axis=1)
    contract = (((0,), (0,)), ((), ()))
    row_partial = lax.dot_general(row_attn, flat_grad, contract, preferred_element_type=jnp.float32)
    col_partial = lax.dot_general(col_attn, flat_grad, contract, preferred_element_type=jnp.float32)
    partial = jnp.concatenate([row_partial, col_partial], axis=0)

    by_rows_of = (((1,), (1,)), ((), ()))
    row_grad = lax.dot_general(
        flat_grad, weight[:half], by_rows_of, preferred_element_type=jnp.float32
    ).astype(jnp.bfloat16)
    partial, col_weight = lax.optimization_barrier((partial, weight[half:]))
    col_grad = lax.dot_general(
        flat_grad, col_weight, by_rows_of, preferred_element_type=jnp.float32
    ).astype(jnp.bfloat16)
    grad_col_part = chunked(col_grad)
    devices_all = lax.axis_size(("dp", "seq"))
    wo_grad = lax.psum_scatter(
        partial.astype(jnp.bfloat16), ("dp", "seq"), scatter_dimension=0, tiled=True
    ).astype(jnp.float32) * (1.0 / math.sqrt(tokens * devices_all))

    col_grads_back = []
    for j in range(chunks):
        grad_cols = lax.all_to_all(
            grad_col_part[j], "seq", split_axis=0, concat_axis=0, tiled=True
        ).reshape(rows, piece, heads_half, DH)
        col_q, col_k, col_v, col_out, col_scores, col_total = col_state[j]
        col_grads = column_backward(
            col_q, col_k, col_v, col_out, grad_cols, col_scores, col_total, col_ok
        )
        col_grads_back.append(
            lax.all_to_all(
                jnp.stack([g.reshape(rows, piece, half) for g in col_grads]),
                "seq",
                split_axis=1,
                concat_axis=1,
                tiled=True,
            )
        )
    col_grads_whole = jnp.stack(col_grads_back, axis=2).reshape(3, tokens, half)

    row_grads = row_backward(
        row_q,
        row_k,
        row_v,
        row_out,
        row_grad.reshape(tokens, heads_half, DH),
        row_scores,
        row_total,
        row_ok,
    )

    layer_out = jnp.dot(attention, weight, preferred_element_type=jnp.float32).astype(
        jnp.bfloat16
    )

    grads = [
        jnp.concatenate([row_grads[i].reshape(tokens, half), col_grads_whole[i]], axis=1)[
            None, None
        ]
        for i in range(3)
    ]
    return (layer_out[None, None], grads[0], grads[1], grads[2], wo_grad)


def solution(mesh):
    in_specs = (
        P("dp", "seq", None, None),
        P("dp", "seq", None, None),
        P("dp", "seq", None, None),
        P("dp", "seq", None, None),
        P("dp", None),
        P(),
        P(),
    )
    out_specs = (
        P("dp", "seq", None, None),
        P("dp", "seq", None, None),
        P("dp", "seq", None, None),
        P("dp", "seq", None, None),
        P(("dp", "seq"), None),
    )
    return jax.shard_map(
        on_device, mesh=mesh, in_specs=in_specs, out_specs=out_specs, check_vma=False
    )
```

```python
import math

import jax
import jax.numpy as jnp
from jax import lax
from jax.sharding import PartitionSpec as P

DH = 128
COLS = 512
BLK = 128

masked_out = -1e30
scale = 1.0 / math.sqrt(DH)


def row_permit(row_mask):
    spread = jnp.repeat(jnp.repeat(row_mask, BLK, axis=0), BLK, axis=1)
    row_index = lax.broadcasted_iota(jnp.int32, (COLS, COLS), 0)
    col_index = lax.broadcasted_iota(jnp.int32, (COLS, COLS), 1)
    return (spread == 1) & (col_index <= row_index)


def softmax_parts(scores, allowed):
    highest = jnp.max(jnp.where(allowed, scores, masked_out), axis=-1, keepdims=True)
    attend = jnp.exp(jnp.where(allowed, scores - highest, masked_out))
    totals = jnp.sum(attend, axis=-1, keepdims=True)
    probs = (attend / totals).astype(jnp.bfloat16)
    return probs, highest + jnp.log(totals)


def row_forward(q, k, v, allowed):
    scores = jnp.einsum("ihd,jhd->hij", q, k, preferred_element_type=jnp.float32) * scale
    probs, log_total = softmax_parts(scores, allowed[None])
    out = jnp.einsum("hij,jhd->ihd", probs, v, preferred_element_type=jnp.float32)
    return out.astype(jnp.bfloat16), scores, log_total


def row_backward(q, k, v, out, grad, scores, log_total, allowed):
    grad_dot = jnp.einsum("ihd,ihd->hi", grad, out, preferred_element_type=jnp.float32)
    back = jnp.where(allowed[None], jnp.exp(scores - log_total), 0.0)
    value_grad = jnp.einsum(
        "hij,ihd->jhd", back.astype(jnp.bfloat16), grad, preferred_element_type=jnp.float32
    )
    prob_grad = jnp.einsum("ihd,jhd->hij", grad, v, preferred_element_type=jnp.float32)
    score_grad = (back * (prob_grad - grad_dot[..., None])).astype(jnp.bfloat16)
    query_grad = jnp.einsum("hij,jhd->ihd", score_grad, k, preferred_element_type=jnp.float32)
    key_grad = jnp.einsum("hij,ihd->jhd", score_grad, q, preferred_element_type=jnp.float32)
    return tuple(
        g.astype(jnp.bfloat16) for g in (query_grad * scale, key_grad * scale, value_grad)
    )


def column_forward(q, k, v, allowed):
    scores = jnp.einsum("rchd,schd->chrs", q, k, preferred_element_type=jnp.float32) * scale
    probs, log_total = softmax_parts(scores, allowed)
    out = jnp.einsum("chrs,schd->rchd", probs, v, preferred_element_type=jnp.float32)
    return out.astype(jnp.bfloat16), scores, log_total


def column_backward(q, k, v, out, grad, scores, log_total, allowed):
    grad_dot = jnp.einsum("rchd,rchd->chr", grad, out, preferred_element_type=jnp.float32)
    back = jnp.where(allowed, jnp.exp(scores - log_total), 0.0)
    value_grad = jnp.einsum(
        "chrs,rchd->schd", back.astype(jnp.bfloat16), grad, preferred_element_type=jnp.float32
    )
    prob_grad = jnp.einsum("rchd,schd->chrs", grad, v, preferred_element_type=jnp.float32)
    score_grad = (back * (prob_grad - grad_dot[..., None])).astype(jnp.bfloat16)
    query_grad = jnp.einsum("chrs,schd->rchd", score_grad, k, preferred_element_type=jnp.float32)
    key_grad = jnp.einsum("chrs,rchd->schd", score_grad, q, preferred_element_type=jnp.float32)
    return tuple(
        g.astype(jnp.bfloat16) for g in (query_grad * scale, key_grad * scale, value_grad)
    )


def on_device(queries, keys, values, out_grad, out_weight, row_mask, col_mask):
    tokens, features = queries.shape[2], queries.shape[3]
    half = features // 2
    heads_half = half // DH
    rows = lax.axis_size("seq")
    cols_each = tokens // rows

    weight = lax.all_gather(out_weight, "dp", axis=0, tiled=True)

    chunks = 2
    piece = cols_each // chunks

    def chunked(t):
        return t.reshape(rows, chunks, piece, half).transpose(1, 0, 2, 3)

    packed = jnp.stack([chunked(t[0, 0, :, half:]) for t in (queries, keys, values)], axis=1)
    col_ok = col_mask == 1
    shipped_all = [
        lax.all_to_all(packed[j], "seq", split_axis=1, concat_axis=1, tiled=True)
        for j in range(chunks)
    ]

    row_ok = row_permit(row_mask)
    split = lambda t: t[0, 0, :, :half].reshape(tokens, heads_half, DH)
    row_q, row_k, row_v = split(queries), split(keys), split(values)
    row_out, row_scores, row_total = row_forward(row_q, row_k, row_v, row_ok)
    row_attn = row_out.reshape(tokens, half)
    flat_grad = out_grad[0, 0]
    contract = (((0,), (0,)), ((), ()))
    row_partial = lax.dot_general(row_attn, flat_grad, contract, preferred_element_type=jnp.float32)
    row_done, shipped_first = lax.optimization_barrier(
        ((row_out, row_scores, row_total, row_partial), shipped_all[0])
    )
    row_out, row_scores, row_total, row_partial = row_done
    row_attn = row_out.reshape(tokens, half)
    shipped_all[0] = shipped_first

    col_state = []
    col_back = []
    for j in range(chunks):
        shipped = shipped_all[j]
        col_q, col_k, col_v = (
            shipped[i].reshape(rows, piece, heads_half, DH) for i in range(3)
        )
        col_out, col_scores, col_total = column_forward(col_q, col_k, col_v, col_ok)
        col_state.append((col_q, col_k, col_v, col_out, col_scores, col_total))
        col_back.append(
            lax.all_to_all(
                col_out.reshape(rows, piece, half), "seq", split_axis=0, concat_axis=0, tiled=True
            )
        )
    col_attn = jnp.stack(col_back, axis=1).reshape(tokens, half)

    attention = jnp.concatenate([row_attn, col_attn], axis=1)
    col_partial = lax.dot_general(col_attn, flat_grad, contract, preferred_element_type=jnp.float32)
    partial = jnp.concatenate([row_partial, col_partial], axis=0)

    by_rows_of = (((1,), (1,)), ((), ()))
    row_grad = lax.dot_general(
        flat_grad, weight[:half], by_rows_of, preferred_element_type=jnp.float32
    ).astype(jnp.bfloat16)
    partial, late_weight = lax.optimization_barrier((partial, weight))
    col_grad = lax.dot_general(
        flat_grad, late_weight[half:], by_rows_of, preferred_element_type=jnp.float32
    ).astype(jnp.bfloat16)
    grad_col_part = chunked(col_grad)
    devices_all = lax.axis_size(("dp", "seq"))
    wo_grad = lax.psum_scatter(
        partial.astype(jnp.bfloat16), ("dp", "seq"), scatter_dimension=0, tiled=True
    ).astype(jnp.float32) * (1.0 / math.sqrt(tokens * devices_all))

    col_grads_back = []
    for j in range(chunks):
        grad_cols = lax.all_to_all(
            grad_col_part[j], "seq", split_axis=0, concat_axis=0, tiled=True
        ).reshape(rows, piece, heads_half, DH)
        col_q, col_k, col_v, col_out, col_scores, col_total = col_state[j]
        col_grads = column_backward(
            col_q, col_k, col_v, col_out, grad_cols, col_scores, col_total, col_ok
        )
        col_grads_back.append(
            lax.all_to_all(
                jnp.stack([g.reshape(rows, piece, half) for g in col_grads]),
                "seq",
                split_axis=1,
                concat_axis=1,
                tiled=True,
            )
        )
    col_grads_whole = jnp.stack(col_grads_back, axis=2).reshape(3, tokens, half)

    row_grads = row_backward(
        row_q,
        row_k,
        row_v,
        row_out,
        row_grad.reshape(tokens, heads_half, DH),
        row_scores,
        row_total,
        row_ok,
    )

    layer_out = jnp.dot(attention, weight, preferred_element_type=jnp.float32).astype(
        jnp.bfloat16
    )

    grads = [
        jnp.concatenate([row_grads[i].reshape(tokens, half), col_grads_whole[i]], axis=1)[
            None, None
        ]
        for i in range(3)
    ]
    return (layer_out[None, None], grads[0], grads[1], grads[2], wo_grad)


def solution(mesh):
    in_specs = (
        P("dp", "seq", None, None),
        P("dp", "seq", None, None),
        P("dp", "seq", None, None),
        P("dp", "seq", None, None),
        P("dp", None),
        P(),
        P(),
    )
    out_specs = (
        P("dp", "seq", None, None),
        P("dp", "seq", None, None),
        P("dp", "seq", None, None),
        P("dp", "seq", None, None),
        P(("dp", "seq"), None),
    )
    return jax.shard_map(
        on_device, mesh=mesh, in_specs=in_specs, out_specs=out_specs, check_vma=False
    )
```

```python
import math

import jax
import jax.numpy as jnp
from jax import lax
from jax.sharding import PartitionSpec as P

DH = 128
COLS = 512
BLK = 128

masked_out = -1e30
scale = 1.0 / math.sqrt(DH)


def row_permit(row_mask):
    spread = jnp.repeat(jnp.repeat(row_mask, BLK, axis=0), BLK, axis=1)
    row_index = lax.broadcasted_iota(jnp.int32, (COLS, COLS), 0)
    col_index = lax.broadcasted_iota(jnp.int32, (COLS, COLS), 1)
    return (spread == 1) & (col_index <= row_index)


def softmax_parts(scores, allowed):
    highest = jnp.max(jnp.where(allowed, scores, masked_out), axis=-1, keepdims=True)
    attend = jnp.exp(jnp.where(allowed, scores - highest, masked_out))
    totals = jnp.sum(attend, axis=-1, keepdims=True)
    probs = (attend / totals).astype(jnp.bfloat16)
    return probs, highest + jnp.log(totals)


def row_forward(q, k, v, allowed):
    scores = jnp.einsum("ihd,jhd->hij", q, k, preferred_element_type=jnp.float32) * scale
    probs, log_total = softmax_parts(scores, allowed[None])
    out = jnp.einsum("hij,jhd->ihd", probs, v, preferred_element_type=jnp.float32)
    return out.astype(jnp.bfloat16), scores, log_total


def row_backward(q, k, v, out, grad, scores, log_total, allowed):
    grad_dot = jnp.einsum("ihd,ihd->hi", grad, out, preferred_element_type=jnp.float32)
    back = jnp.where(allowed[None], jnp.exp(scores - log_total), 0.0)
    value_grad = jnp.einsum(
        "hij,ihd->jhd", back.astype(jnp.bfloat16), grad, preferred_element_type=jnp.float32
    )
    prob_grad = jnp.einsum("ihd,jhd->hij", grad, v, preferred_element_type=jnp.float32)
    score_grad = (back * (prob_grad - grad_dot[..., None])).astype(jnp.bfloat16)
    query_grad = jnp.einsum("hij,jhd->ihd", score_grad, k, preferred_element_type=jnp.float32)
    key_grad = jnp.einsum("hij,ihd->jhd", score_grad, q, preferred_element_type=jnp.float32)
    return tuple(
        g.astype(jnp.bfloat16) for g in (query_grad * scale, key_grad * scale, value_grad)
    )


def column_forward(q, k, v, allowed):
    scores = jnp.einsum("rchd,schd->chrs", q, k, preferred_element_type=jnp.float32) * scale
    probs, log_total = softmax_parts(scores, allowed)
    out = jnp.einsum("chrs,schd->rchd", probs, v, preferred_element_type=jnp.float32)
    return out.astype(jnp.bfloat16), scores, log_total


def column_backward(q, k, v, out, grad, scores, log_total, allowed):
    grad_dot = jnp.einsum("rchd,rchd->chr", grad, out, preferred_element_type=jnp.float32)
    back = jnp.where(allowed, jnp.exp(scores - log_total), 0.0)
    value_grad = jnp.einsum(
        "chrs,rchd->schd", back.astype(jnp.bfloat16), grad, preferred_element_type=jnp.float32
    )
    prob_grad = jnp.einsum("rchd,schd->chrs", grad, v, preferred_element_type=jnp.float32)
    score_grad = (back * (prob_grad - grad_dot[..., None])).astype(jnp.bfloat16)
    query_grad = jnp.einsum("chrs,schd->rchd", score_grad, k, preferred_element_type=jnp.float32)
    key_grad = jnp.einsum("chrs,rchd->schd", score_grad, q, preferred_element_type=jnp.float32)
    return tuple(
        g.astype(jnp.bfloat16) for g in (query_grad * scale, key_grad * scale, value_grad)
    )


def on_device(queries, keys, values, out_grad, out_weight, row_mask, col_mask):
    tokens, features = queries.shape[2], queries.shape[3]
    half = features // 2
    heads_half = half // DH
    rows = lax.axis_size("seq")
    cols_each = tokens // rows

    weight = lax.all_gather(out_weight, "dp", axis=0, tiled=True)

    chunks = 2
    piece = cols_each // chunks

    def chunked(t):
        return t.reshape(rows, chunks, piece, half).transpose(1, 0, 2, 3)

    packed = jnp.stack([chunked(t[0, 0, :, half:]) for t in (queries, keys, values)], axis=1)
    col_ok = col_mask == 1
    shipped_all = [
        lax.all_to_all(packed[j], "seq", split_axis=1, concat_axis=1, tiled=True)
        for j in range(chunks)
    ]

    row_ok = row_permit(row_mask)
    split = lambda t: t[0, 0, :, :half].reshape(tokens, heads_half, DH)
    row_q, row_k, row_v = split(queries), split(keys), split(values)
    row_out, row_scores, row_total = row_forward(row_q, row_k, row_v, row_ok)
    row_attn = row_out.reshape(tokens, half)
    flat_grad = out_grad[0, 0]
    contract = (((0,), (0,)), ((), ()))
    row_done, shipped_first = lax.optimization_barrier(
        ((row_out, row_scores, row_total), shipped_all[0])
    )
    row_out, row_scores, row_total = row_done
    row_attn = row_out.reshape(tokens, half)
    shipped_all[0] = shipped_first

    col_state = []
    col_back = []
    for j in range(chunks):
        shipped = shipped_all[j]
        col_q, col_k, col_v = (
            shipped[i].reshape(rows, piece, heads_half, DH) for i in range(3)
        )
        col_out, col_scores, col_total = column_forward(col_q, col_k, col_v, col_ok)
        col_state.append((col_q, col_k, col_v, col_out, col_scores, col_total))
        col_back.append(col_out.reshape(rows, piece, half))
    col_attn = lax.all_to_all(
        jnp.stack(col_back, axis=1), "seq", split_axis=0, concat_axis=0, tiled=True
    ).reshape(tokens, half)

    attention = jnp.concatenate([row_attn, col_attn], axis=1)
    partial = lax.dot_general(attention, flat_grad, contract, preferred_element_type=jnp.float32)

    by_rows_of = (((1,), (1,)), ((), ()))
    row_grad = lax.dot_general(
        flat_grad, weight[:half], by_rows_of, preferred_element_type=jnp.float32
    ).astype(jnp.bfloat16)
    partial, late_weight = lax.optimization_barrier((partial, weight))
    col_grad = lax.dot_general(
        flat_grad, late_weight[half:], by_rows_of, preferred_element_type=jnp.float32
    ).astype(jnp.bfloat16)
    grad_col_part = chunked(col_grad)
    devices_all = lax.axis_size(("dp", "seq"))
    wo_grad = lax.psum_scatter(
        partial.astype(jnp.bfloat16), ("dp", "seq"), scatter_dimension=0, tiled=True
    ).astype(jnp.float32) * (1.0 / math.sqrt(tokens * devices_all))

    col_grads_back = []
    for j in range(chunks):
        grad_cols = lax.all_to_all(
            grad_col_part[j], "seq", split_axis=0, concat_axis=0, tiled=True
        ).reshape(rows, piece, heads_half, DH)
        col_q, col_k, col_v, col_out, col_scores, col_total = col_state[j]
        col_grads = column_backward(
            col_q, col_k, col_v, col_out, grad_cols, col_scores, col_total, col_ok
        )
        col_grads_back.append(
            lax.all_to_all(
                jnp.stack([g.reshape(rows, piece, half) for g in col_grads]),
                "seq",
                split_axis=1,
                concat_axis=1,
                tiled=True,
            )
        )
    col_grads_whole = jnp.stack(col_grads_back, axis=2).reshape(3, tokens, half)

    row_grads = row_backward(
        row_q,
        row_k,
        row_v,
        row_out,
        row_grad.reshape(tokens, heads_half, DH),
        row_scores,
        row_total,
        row_ok,
    )

    layer_out = jnp.dot(attention, weight, preferred_element_type=jnp.float32).astype(
        jnp.bfloat16
    )

    grads = [
        jnp.concatenate([row_grads[i].reshape(tokens, half), col_grads_whole[i]], axis=1)[
            None, None
        ]
        for i in range(3)
    ]
    return (layer_out[None, None], grads[0], grads[1], grads[2], wo_grad)


def solution(mesh):
    in_specs = (
        P("dp", "seq", None, None),
        P("dp", "seq", None, None),
        P("dp", "seq", None, None),
        P("dp", "seq", None, None),
        P("dp", None),
        P(),
        P(),
    )
    out_specs = (
        P("dp", "seq", None, None),
        P("dp", "seq", None, None),
        P("dp", "seq", None, None),
        P("dp", "seq", None, None),
        P(("dp", "seq"), None),
    )
    return jax.shard_map(
        on_device, mesh=mesh, in_specs=in_specs, out_specs=out_specs, check_vma=False
    )
```

```python
import math

import jax
import jax.numpy as jnp
from jax import lax
from jax.sharding import PartitionSpec as P

DH = 128
COLS = 512
BLK = 128

masked_out = -1e30
scale = 1.0 / math.sqrt(DH)


def row_permit(row_mask):
    spread = jnp.repeat(jnp.repeat(row_mask, BLK, axis=0), BLK, axis=1)
    row_index = lax.broadcasted_iota(jnp.int32, (COLS, COLS), 0)
    col_index = lax.broadcasted_iota(jnp.int32, (COLS, COLS), 1)
    return (spread == 1) & (col_index <= row_index)


def softmax_parts(scores, allowed):
    highest = jnp.max(jnp.where(allowed, scores, masked_out), axis=-1, keepdims=True)
    attend = jnp.exp(jnp.where(allowed, scores - highest, masked_out))
    totals = jnp.sum(attend, axis=-1, keepdims=True)
    probs = (attend / totals).astype(jnp.bfloat16)
    return probs, highest + jnp.log(totals)


def row_forward(q, k, v, allowed):
    scores = jnp.einsum("ihd,jhd->hij", q, k, preferred_element_type=jnp.float32) * scale
    probs, log_total = softmax_parts(scores, allowed[None])
    out = jnp.einsum("hij,jhd->ihd", probs, v, preferred_element_type=jnp.float32)
    return out.astype(jnp.bfloat16), scores, log_total


def row_backward(q, k, v, out, grad, scores, log_total, allowed):
    grad_dot = jnp.einsum("ihd,ihd->hi", grad, out, preferred_element_type=jnp.float32)
    back = jnp.where(allowed[None], jnp.exp(scores - log_total), 0.0)
    value_grad = jnp.einsum(
        "hij,ihd->jhd", back.astype(jnp.bfloat16), grad, preferred_element_type=jnp.float32
    )
    prob_grad = jnp.einsum("ihd,jhd->hij", grad, v, preferred_element_type=jnp.float32)
    score_grad = (back * (prob_grad - grad_dot[..., None])).astype(jnp.bfloat16)
    query_grad = jnp.einsum("hij,jhd->ihd", score_grad, k, preferred_element_type=jnp.float32)
    key_grad = jnp.einsum("hij,ihd->jhd", score_grad, q, preferred_element_type=jnp.float32)
    return tuple(
        g.astype(jnp.bfloat16) for g in (query_grad * scale, key_grad * scale, value_grad)
    )


def column_forward(q, k, v, allowed):
    scores = jnp.einsum("rchd,schd->chrs", q, k, preferred_element_type=jnp.float32) * scale
    probs, log_total = softmax_parts(scores, allowed)
    out = jnp.einsum("chrs,schd->rchd", probs, v, preferred_element_type=jnp.float32)
    return out.astype(jnp.bfloat16), scores, log_total


def column_backward(q, k, v, out, grad, scores, log_total, allowed):
    grad_dot = jnp.einsum("rchd,rchd->chr", grad, out, preferred_element_type=jnp.float32)
    back = jnp.where(allowed, jnp.exp(scores - log_total), 0.0)
    value_grad = jnp.einsum(
        "chrs,rchd->schd", back.astype(jnp.bfloat16), grad, preferred_element_type=jnp.float32
    )
    prob_grad = jnp.einsum("rchd,schd->chrs", grad, v, preferred_element_type=jnp.float32)
    score_grad = (back * (prob_grad - grad_dot[..., None])).astype(jnp.bfloat16)
    query_grad = jnp.einsum("chrs,schd->rchd", score_grad, k, preferred_element_type=jnp.float32)
    key_grad = jnp.einsum("chrs,rchd->schd", score_grad, q, preferred_element_type=jnp.float32)
    return tuple(
        g.astype(jnp.bfloat16) for g in (query_grad * scale, key_grad * scale, value_grad)
    )


def on_device(queries, keys, values, out_grad, out_weight, row_mask, col_mask):
    tokens, features = queries.shape[2], queries.shape[3]
    half = features // 2
    heads_half = half // DH
    rows = lax.axis_size("seq")
    cols_each = tokens // rows

    weight = lax.all_gather(out_weight, "dp", axis=0, tiled=True)

    chunks = 2
    piece = cols_each // chunks

    def chunked(t):
        return t.reshape(rows, chunks, piece, half).transpose(1, 0, 2, 3)

    packed = jnp.stack([chunked(t[0, 0, :, half:]) for t in (queries, keys, values)], axis=1)
    col_ok = col_mask == 1
    shipped_all = [
        lax.all_to_all(packed[j], "seq", split_axis=1, concat_axis=1, tiled=True)
        for j in range(chunks)
    ]

    row_ok = row_permit(row_mask)
    split = lambda t: t[0, 0, :, :half].reshape(tokens, heads_half, DH)
    row_q, row_k, row_v = split(queries), split(keys), split(values)
    row_out, row_scores, row_total = row_forward(row_q, row_k, row_v, row_ok)
    row_attn = row_out.reshape(tokens, half)
    flat_grad = out_grad[0, 0]
    contract = (((0,), (0,)), ((), ()))
    row_done, shipped_first = lax.optimization_barrier(
        ((row_out, row_scores, row_total), shipped_all[0])
    )
    row_out, row_scores, row_total = row_done
    row_attn = row_out.reshape(tokens, half)
    shipped_all[0] = shipped_first

    col_state = []
    col_back = []
    for j in range(chunks):
        shipped = shipped_all[j]
        if j > 0:
            done_before, shipped = lax.optimization_barrier((col_state[j - 1], shipped))
            col_state[j - 1] = done_before
            col_back[j - 1] = done_before[3].reshape(rows, piece, half)
        col_q, col_k, col_v = (
            shipped[i].reshape(rows, piece, heads_half, DH) for i in range(3)
        )
        col_out, col_scores, col_total = column_forward(col_q, col_k, col_v, col_ok)
        col_state.append((col_q, col_k, col_v, col_out, col_scores, col_total))
        col_back.append(col_out.reshape(rows, piece, half))
    col_attn = lax.all_to_all(
        jnp.stack(col_back, axis=1), "seq", split_axis=0, concat_axis=0, tiled=True
    ).reshape(tokens, half)

    attention = jnp.concatenate([row_attn, col_attn], axis=1)
    partial = lax.dot_general(attention, flat_grad, contract, preferred_element_type=jnp.float32)

    by_rows_of = (((1,), (1,)), ((), ()))
    row_grad = lax.dot_general(
        flat_grad, weight[:half], by_rows_of, preferred_element_type=jnp.float32
    ).astype(jnp.bfloat16)
    partial, late_weight = lax.optimization_barrier((partial, weight))
    col_grad = lax.dot_general(
        flat_grad, late_weight[half:], by_rows_of, preferred_element_type=jnp.float32
    ).astype(jnp.bfloat16)
    grad_col_part = chunked(col_grad)
    devices_all = lax.axis_size(("dp", "seq"))
    wo_grad = lax.psum_scatter(
        partial.astype(jnp.bfloat16), ("dp", "seq"), scatter_dimension=0, tiled=True
    ).astype(jnp.float32) * (1.0 / math.sqrt(tokens * devices_all))

    col_grads_back = []
    for j in range(chunks):
        grad_cols = lax.all_to_all(
            grad_col_part[j], "seq", split_axis=0, concat_axis=0, tiled=True
        ).reshape(rows, piece, heads_half, DH)
        col_q, col_k, col_v, col_out, col_scores, col_total = col_state[j]
        col_grads = column_backward(
            col_q, col_k, col_v, col_out, grad_cols, col_scores, col_total, col_ok
        )
        col_grads_back.append(
            lax.all_to_all(
                jnp.stack([g.reshape(rows, piece, half) for g in col_grads]),
                "seq",
                split_axis=1,
                concat_axis=1,
                tiled=True,
            )
        )
    col_grads_whole = jnp.stack(col_grads_back, axis=2).reshape(3, tokens, half)

    row_grads = row_backward(
        row_q,
        row_k,
        row_v,
        row_out,
        row_grad.reshape(tokens, heads_half, DH),
        row_scores,
        row_total,
        row_ok,
    )

    layer_out = jnp.dot(attention, weight, preferred_element_type=jnp.float32).astype(
        jnp.bfloat16
    )

    grads = [
        jnp.concatenate([row_grads[i].reshape(tokens, half), col_grads_whole[i]], axis=1)[
            None, None
        ]
        for i in range(3)
    ]
    return (layer_out[None, None], grads[0], grads[1], grads[2], wo_grad)


def solution(mesh):
    in_specs = (
        P("dp", "seq", None, None),
        P("dp", "seq", None, None),
        P("dp", "seq", None, None),
        P("dp", "seq", None, None),
        P("dp", None),
        P(),
        P(),
    )
    out_specs = (
        P("dp", "seq", None, None),
        P("dp", "seq", None, None),
        P("dp", "seq", None, None),
        P("dp", "seq", None, None),
        P(("dp", "seq"), None),
    )
    return jax.shard_map(
        on_device, mesh=mesh, in_specs=in_specs, out_specs=out_specs, check_vma=False
    )
```

```python
import math

import jax
import jax.numpy as jnp
from jax import lax
from jax.sharding import PartitionSpec as P

DH = 128
COLS = 512
BLK = 128

masked_out = -1e30
scale = 1.0 / math.sqrt(DH)


def row_permit(row_mask):
    spread = jnp.repeat(jnp.repeat(row_mask, BLK, axis=0), BLK, axis=1)
    row_index = lax.broadcasted_iota(jnp.int32, (COLS, COLS), 0)
    col_index = lax.broadcasted_iota(jnp.int32, (COLS, COLS), 1)
    return (spread == 1) & (col_index <= row_index)


def softmax_parts(scores, allowed):
    highest = jnp.max(jnp.where(allowed, scores, masked_out), axis=-1, keepdims=True)
    attend = jnp.exp(jnp.where(allowed, scores - highest, masked_out))
    totals = jnp.sum(attend, axis=-1, keepdims=True)
    probs = (attend / totals).astype(jnp.bfloat16)
    return probs, highest + jnp.log(totals)


def row_forward(q, k, v, allowed):
    scores = jnp.einsum("ihd,jhd->hij", q, k, preferred_element_type=jnp.float32) * scale
    probs, log_total = softmax_parts(scores, allowed[None])
    out = jnp.einsum("hij,jhd->ihd", probs, v, preferred_element_type=jnp.float32)
    return out.astype(jnp.bfloat16), scores, log_total


def row_backward(q, k, v, out, grad, scores, log_total, allowed):
    grad_dot = jnp.einsum("ihd,ihd->hi", grad, out, preferred_element_type=jnp.float32)
    back = jnp.where(allowed[None], jnp.exp(scores - log_total), 0.0)
    value_grad = jnp.einsum(
        "hij,ihd->jhd", back.astype(jnp.bfloat16), grad, preferred_element_type=jnp.float32
    )
    prob_grad = jnp.einsum("ihd,jhd->hij", grad, v, preferred_element_type=jnp.float32)
    score_grad = (back * (prob_grad - grad_dot[..., None])).astype(jnp.bfloat16)
    query_grad = jnp.einsum("hij,jhd->ihd", score_grad, k, preferred_element_type=jnp.float32)
    key_grad = jnp.einsum("hij,ihd->jhd", score_grad, q, preferred_element_type=jnp.float32)
    return tuple(
        g.astype(jnp.bfloat16) for g in (query_grad * scale, key_grad * scale, value_grad)
    )


def column_forward(q, k, v, allowed):
    f32 = jnp.float32
    scores = jnp.sum(q.astype(f32)[:, None] * k.astype(f32)[None], axis=-1) * scale
    permit = allowed[:, :, None, None]
    highest = jnp.max(jnp.where(permit, scores, masked_out), axis=1, keepdims=True)
    attend = jnp.exp(jnp.where(permit, scores - highest, masked_out))
    totals = jnp.sum(attend, axis=1, keepdims=True)
    probs = (attend / totals).astype(jnp.bfloat16)
    out = jnp.sum(probs.astype(f32)[..., None] * v.astype(f32)[None], axis=1)
    return out.astype(jnp.bfloat16), scores, highest + jnp.log(totals)


def column_backward(q, k, v, out, grad, scores, log_total, allowed):
    f32 = jnp.float32
    qf, kf, vf, gf = (t.astype(f32) for t in (q, k, v, grad))
    grad_dot = jnp.sum(gf * out.astype(f32), axis=-1)
    back = jnp.where(allowed[:, :, None, None], jnp.exp(scores - log_total), 0.0)
    value_grad = jnp.sum(back.astype(jnp.bfloat16).astype(f32)[..., None] * gf[:, None], axis=0)
    prob_grad = jnp.sum(gf[:, None] * vf[None], axis=-1)
    score_grad = (back * (prob_grad - grad_dot[:, None])).astype(jnp.bfloat16).astype(f32)
    query_grad = jnp.sum(score_grad[..., None] * kf[None], axis=1)
    key_grad = jnp.sum(score_grad[..., None] * qf[:, None], axis=0)
    return tuple(
        g.astype(jnp.bfloat16) for g in (query_grad * scale, key_grad * scale, value_grad)
    )


def on_device(queries, keys, values, out_grad, out_weight, row_mask, col_mask):
    tokens, features = queries.shape[2], queries.shape[3]
    half = features // 2
    heads_half = half // DH
    rows = lax.axis_size("seq")
    cols_each = tokens // rows

    weight = lax.all_gather(out_weight, "dp", axis=0, tiled=True)

    chunks = 2
    piece = cols_each // chunks

    def chunked(t):
        return t.reshape(rows, chunks, piece, half).transpose(1, 0, 2, 3)

    packed = jnp.stack([chunked(t[0, 0, :, half:]) for t in (queries, keys, values)], axis=1)
    col_ok = col_mask == 1
    shipped_all = [
        lax.all_to_all(packed[j], "seq", split_axis=1, concat_axis=1, tiled=True)
        for j in range(chunks)
    ]

    row_ok = row_permit(row_mask)
    split = lambda t: t[0, 0, :, :half].reshape(tokens, heads_half, DH)
    row_q, row_k, row_v = split(queries), split(keys), split(values)
    row_out, row_scores, row_total = row_forward(row_q, row_k, row_v, row_ok)
    row_attn = row_out.reshape(tokens, half)
    flat_grad = out_grad[0, 0]
    contract = (((0,), (0,)), ((), ()))
    row_done, shipped_first = lax.optimization_barrier(
        ((row_out, row_scores, row_total), shipped_all[0])
    )
    row_out, row_scores, row_total = row_done
    row_attn = row_out.reshape(tokens, half)
    shipped_all[0] = shipped_first

    col_state = []
    col_back = []
    for j in range(chunks):
        shipped = shipped_all[j]
        if j > 0:
            done_before, shipped = lax.optimization_barrier((col_state[j - 1], shipped))
            col_state[j - 1] = done_before
            col_back[j - 1] = done_before[3].reshape(rows, piece, half)
        col_q, col_k, col_v = (
            shipped[i].reshape(rows, piece, heads_half, DH) for i in range(3)
        )
        col_out, col_scores, col_total = column_forward(col_q, col_k, col_v, col_ok)
        col_state.append((col_q, col_k, col_v, col_out, col_scores, col_total))
        col_back.append(col_out.reshape(rows, piece, half))
    col_attn = lax.all_to_all(
        jnp.stack(col_back, axis=1), "seq", split_axis=0, concat_axis=0, tiled=True
    ).reshape(tokens, half)

    attention = jnp.concatenate([row_attn, col_attn], axis=1)
    partial = lax.dot_general(attention, flat_grad, contract, preferred_element_type=jnp.float32)

    by_rows_of = (((1,), (1,)), ((), ()))
    row_grad = lax.dot_general(
        flat_grad, weight[:half], by_rows_of, preferred_element_type=jnp.float32
    ).astype(jnp.bfloat16)
    partial, late_weight = lax.optimization_barrier((partial, weight))
    col_grad = lax.dot_general(
        flat_grad, late_weight[half:], by_rows_of, preferred_element_type=jnp.float32
    ).astype(jnp.bfloat16)
    grad_col_part = chunked(col_grad)
    devices_all = lax.axis_size(("dp", "seq"))
    wo_grad = lax.psum_scatter(
        partial.astype(jnp.bfloat16), ("dp", "seq"), scatter_dimension=0, tiled=True
    ).astype(jnp.float32) * (1.0 / math.sqrt(tokens * devices_all))

    col_grads_back = []
    for j in range(chunks):
        grad_cols = lax.all_to_all(
            grad_col_part[j], "seq", split_axis=0, concat_axis=0, tiled=True
        ).reshape(rows, piece, heads_half, DH)
        col_q, col_k, col_v, col_out, col_scores, col_total = col_state[j]
        col_grads = column_backward(
            col_q, col_k, col_v, col_out, grad_cols, col_scores, col_total, col_ok
        )
        col_grads_back.append(
            lax.all_to_all(
                jnp.stack([g.reshape(rows, piece, half) for g in col_grads]),
                "seq",
                split_axis=1,
                concat_axis=1,
                tiled=True,
            )
        )
    col_grads_whole = jnp.stack(col_grads_back, axis=2).reshape(3, tokens, half)

    row_grads = row_backward(
        row_q,
        row_k,
        row_v,
        row_out,
        row_grad.reshape(tokens, heads_half, DH),
        row_scores,
        row_total,
        row_ok,
    )

    layer_out = jnp.dot(attention, weight, preferred_element_type=jnp.float32).astype(
        jnp.bfloat16
    )

    grads = [
        jnp.concatenate([row_grads[i].reshape(tokens, half), col_grads_whole[i]], axis=1)[
            None, None
        ]
        for i in range(3)
    ]
    return (layer_out[None, None], grads[0], grads[1], grads[2], wo_grad)


def solution(mesh):
    in_specs = (
        P("dp", "seq", None, None),
        P("dp", "seq", None, None),
        P("dp", "seq", None, None),
        P("dp", "seq", None, None),
        P("dp", None),
        P(),
        P(),
    )
    out_specs = (
        P("dp", "seq", None, None),
        P("dp", "seq", None, None),
        P("dp", "seq", None, None),
        P("dp", "seq", None, None),
        P(("dp", "seq"), None),
    )
    return jax.shard_map(
        on_device, mesh=mesh, in_specs=in_specs, out_specs=out_specs, check_vma=False
    )
```

```python
import math

import jax
import jax.numpy as jnp
from jax import lax
from jax.sharding import PartitionSpec as P

DH = 128
COLS = 512
BLK = 128

masked_out = -1e30
scale = 1.0 / math.sqrt(DH)


def row_permit(row_mask):
    spread = jnp.repeat(jnp.repeat(row_mask, BLK, axis=0), BLK, axis=1)
    row_index = lax.broadcasted_iota(jnp.int32, (COLS, COLS), 0)
    col_index = lax.broadcasted_iota(jnp.int32, (COLS, COLS), 1)
    return (spread == 1) & (col_index <= row_index)


def softmax_parts(scores, allowed):
    highest = jnp.max(jnp.where(allowed, scores, masked_out), axis=-1, keepdims=True)
    attend = jnp.exp(jnp.where(allowed, scores - highest, masked_out))
    totals = jnp.sum(attend, axis=-1, keepdims=True)
    probs = (attend / totals).astype(jnp.bfloat16)
    return probs, highest + jnp.log(totals)


def row_forward(q, k, v, allowed):
    scores = jnp.einsum("ihd,jhd->hij", q, k, preferred_element_type=jnp.float32) * scale
    probs, log_total = softmax_parts(scores, allowed[None])
    out = jnp.einsum("hij,jhd->ihd", probs, v, preferred_element_type=jnp.float32)
    return out.astype(jnp.bfloat16), scores, log_total


def row_backward(q, k, v, out, grad, scores, log_total, allowed):
    grad_dot = jnp.einsum("ihd,ihd->hi", grad, out, preferred_element_type=jnp.float32)
    back = jnp.where(allowed[None], jnp.exp(scores - log_total), 0.0)
    value_grad = jnp.einsum(
        "hij,ihd->jhd", back.astype(jnp.bfloat16), grad, preferred_element_type=jnp.float32
    )
    prob_grad = jnp.einsum("ihd,jhd->hij", grad, v, preferred_element_type=jnp.float32)
    score_grad = (back * (prob_grad - grad_dot[..., None])).astype(jnp.bfloat16)
    query_grad = jnp.einsum("hij,jhd->ihd", score_grad, k, preferred_element_type=jnp.float32)
    key_grad = jnp.einsum("hij,ihd->jhd", score_grad, q, preferred_element_type=jnp.float32)
    return tuple(
        g.astype(jnp.bfloat16) for g in (query_grad * scale, key_grad * scale, value_grad)
    )


def column_forward(q, k, v, allowed):
    scores = jnp.einsum("rchd,schd->chrs", q, k, preferred_element_type=jnp.float32) * scale
    probs, log_total = softmax_parts(scores, allowed)
    out = jnp.einsum("chrs,schd->rchd", probs, v, preferred_element_type=jnp.float32)
    return out.astype(jnp.bfloat16), scores, log_total


def column_backward(q, k, v, out, grad, scores, log_total, allowed):
    grad_dot = jnp.einsum("rchd,rchd->chr", grad, out, preferred_element_type=jnp.float32)
    back = jnp.where(allowed, jnp.exp(scores - log_total), 0.0)
    value_grad = jnp.einsum(
        "chrs,rchd->schd", back.astype(jnp.bfloat16), grad, preferred_element_type=jnp.float32
    )
    prob_grad = jnp.einsum("rchd,schd->chrs", grad, v, preferred_element_type=jnp.float32)
    score_grad = (back * (prob_grad - grad_dot[..., None])).astype(jnp.bfloat16)
    query_grad = jnp.einsum("chrs,schd->rchd", score_grad, k, preferred_element_type=jnp.float32)
    key_grad = jnp.einsum("chrs,rchd->schd", score_grad, q, preferred_element_type=jnp.float32)
    return tuple(
        g.astype(jnp.bfloat16) for g in (query_grad * scale, key_grad * scale, value_grad)
    )


def on_device(queries, keys, values, out_grad, out_weight, row_mask, col_mask):
    tokens, features = queries.shape[2], queries.shape[3]
    half = features // 2
    heads_half = half // DH
    rows = lax.axis_size("seq")
    cols_each = tokens // rows

    weight = lax.all_gather(out_weight, "dp", axis=0, tiled=True)

    bounds = [0, cols_each * 3 // 4, cols_each]
    chunks = len(bounds) - 1
    widths = [bounds[j + 1] - bounds[j] for j in range(chunks)]

    def chunked(t):
        by_dest = t.reshape(rows, cols_each, half)
        return [by_dest[:, bounds[j] : bounds[j + 1]] for j in range(chunks)]

    col_in = [chunked(t[0, 0, :, half:]) for t in (queries, keys, values)]
    col_ok = col_mask == 1
    shipped_all = [
        lax.all_to_all(
            jnp.stack([part[j] for part in col_in]), "seq", split_axis=1, concat_axis=1, tiled=True
        )
        for j in range(chunks)
    ]

    row_ok = row_permit(row_mask)
    split = lambda t: t[0, 0, :, :half].reshape(tokens, heads_half, DH)
    row_q, row_k, row_v = split(queries), split(keys), split(values)
    row_out, row_scores, row_total = row_forward(row_q, row_k, row_v, row_ok)
    row_attn = row_out.reshape(tokens, half)
    flat_grad = out_grad[0, 0]
    contract = (((0,), (0,)), ((), ()))
    row_done, shipped_first = lax.optimization_barrier(
        ((row_out, row_scores, row_total), shipped_all[0])
    )
    row_out, row_scores, row_total = row_done
    row_attn = row_out.reshape(tokens, half)
    shipped_all[0] = shipped_first

    col_state = []
    col_back = []
    for j in range(chunks):
        shipped = shipped_all[j]
        if j > 0:
            done_before, shipped = lax.optimization_barrier((col_state[j - 1], shipped))
            col_state[j - 1] = done_before
            col_back[j - 1] = done_before[3].reshape(rows, widths[j - 1], half)
        col_q, col_k, col_v = (
            shipped[i].reshape(rows, widths[j], heads_half, DH) for i in range(3)
        )
        col_out, col_scores, col_total = column_forward(col_q, col_k, col_v, col_ok)
        col_state.append((col_q, col_k, col_v, col_out, col_scores, col_total))
        col_back.append(col_out.reshape(rows, widths[j], half))
    col_attn = lax.all_to_all(
        jnp.concatenate(col_back, axis=1), "seq", split_axis=0, concat_axis=0, tiled=True
    ).reshape(tokens, half)

    attention = jnp.concatenate([row_attn, col_attn], axis=1)
    partial = lax.dot_general(attention, flat_grad, contract, preferred_element_type=jnp.float32)

    by_rows_of = (((1,), (1,)), ((), ()))
    row_grad = lax.dot_general(
        flat_grad, weight[:half], by_rows_of, preferred_element_type=jnp.float32
    ).astype(jnp.bfloat16)
    partial, late_weight = lax.optimization_barrier((partial, weight))
    col_grad = lax.dot_general(
        flat_grad, late_weight[half:], by_rows_of, preferred_element_type=jnp.float32
    ).astype(jnp.bfloat16)
    grad_col_part = chunked(col_grad)
    devices_all = lax.axis_size(("dp", "seq"))
    wo_grad = lax.psum_scatter(
        partial.astype(jnp.bfloat16), ("dp", "seq"), scatter_dimension=0, tiled=True
    ).astype(jnp.float32) * (1.0 / math.sqrt(tokens * devices_all))

    col_grads_back = []
    for j in range(chunks):
        grad_cols = lax.all_to_all(
            grad_col_part[j], "seq", split_axis=0, concat_axis=0, tiled=True
        ).reshape(rows, widths[j], heads_half, DH)
        col_q, col_k, col_v, col_out, col_scores, col_total = col_state[j]
        col_grads = column_backward(
            col_q, col_k, col_v, col_out, grad_cols, col_scores, col_total, col_ok
        )
        col_grads_back.append(
            lax.all_to_all(
                jnp.stack([g.reshape(rows, widths[j], half) for g in col_grads]),
                "seq",
                split_axis=1,
                concat_axis=1,
                tiled=True,
            )
        )
    col_grads_whole = jnp.concatenate(col_grads_back, axis=2).reshape(3, tokens, half)

    row_grads = row_backward(
        row_q,
        row_k,
        row_v,
        row_out,
        row_grad.reshape(tokens, heads_half, DH),
        row_scores,
        row_total,
        row_ok,
    )

    layer_out = jnp.dot(attention, weight, preferred_element_type=jnp.float32).astype(
        jnp.bfloat16
    )

    grads = [
        jnp.concatenate([row_grads[i].reshape(tokens, half), col_grads_whole[i]], axis=1)[
            None, None
        ]
        for i in range(3)
    ]
    return (layer_out[None, None], grads[0], grads[1], grads[2], wo_grad)


def solution(mesh):
    in_specs = (
        P("dp", "seq", None, None),
        P("dp", "seq", None, None),
        P("dp", "seq", None, None),
        P("dp", "seq", None, None),
        P("dp", None),
        P(),
        P(),
    )
    out_specs = (
        P("dp", "seq", None, None),
        P("dp", "seq", None, None),
        P("dp", "seq", None, None),
        P("dp", "seq", None, None),
        P(("dp", "seq"), None),
    )
    return jax.shard_map(
        on_device, mesh=mesh, in_specs=in_specs, out_specs=out_specs, check_vma=False
    )
```

```python
import math

import jax
import jax.numpy as jnp
from jax import lax
from jax.sharding import PartitionSpec as P

DH = 128
COLS = 512
BLK = 128

masked_out = -1e30
scale = 1.0 / math.sqrt(DH)


def row_permit(row_mask):
    spread = jnp.repeat(jnp.repeat(row_mask, BLK, axis=0), BLK, axis=1)
    row_index = lax.broadcasted_iota(jnp.int32, (COLS, COLS), 0)
    col_index = lax.broadcasted_iota(jnp.int32, (COLS, COLS), 1)
    return (spread == 1) & (col_index <= row_index)


def softmax_parts(scores, allowed):
    highest = jnp.max(jnp.where(allowed, scores, masked_out), axis=-1, keepdims=True)
    attend = jnp.exp(jnp.where(allowed, scores - highest, masked_out))
    totals = jnp.sum(attend, axis=-1, keepdims=True)
    probs = (attend / totals).astype(jnp.bfloat16)
    return probs, highest + jnp.log(totals)


def row_forward(q, k, v, allowed):
    scores = jnp.einsum("ihd,jhd->hij", q, k, preferred_element_type=jnp.float32) * scale
    probs, log_total = softmax_parts(scores, allowed[None])
    out = jnp.einsum("hij,jhd->ihd", probs, v, preferred_element_type=jnp.float32)
    return out.astype(jnp.bfloat16), scores, log_total


def row_backward(q, k, v, out, grad, scores, log_total, allowed):
    grad_dot = jnp.einsum("ihd,ihd->hi", grad, out, preferred_element_type=jnp.float32)
    back = jnp.where(allowed[None], jnp.exp(scores - log_total), 0.0)
    value_grad = jnp.einsum(
        "hij,ihd->jhd", back.astype(jnp.bfloat16), grad, preferred_element_type=jnp.float32
    )
    prob_grad = jnp.einsum("ihd,jhd->hij", grad, v, preferred_element_type=jnp.float32)
    score_grad = (back * (prob_grad - grad_dot[..., None])).astype(jnp.bfloat16)
    query_grad = jnp.einsum("hij,jhd->ihd", score_grad, k, preferred_element_type=jnp.float32)
    key_grad = jnp.einsum("hij,ihd->jhd", score_grad, q, preferred_element_type=jnp.float32)
    return tuple(
        g.astype(jnp.bfloat16) for g in (query_grad * scale, key_grad * scale, value_grad)
    )


def column_forward(q, k, v, allowed):
    scores = jnp.einsum("rchd,schd->chrs", q, k, preferred_element_type=jnp.float32) * scale
    probs, log_total = softmax_parts(scores, allowed)
    out = jnp.einsum("chrs,schd->rchd", probs, v, preferred_element_type=jnp.float32)
    return out.astype(jnp.bfloat16), scores, log_total


def column_backward(q, k, v, out, grad, scores, log_total, allowed):
    grad_dot = jnp.einsum("rchd,rchd->chr", grad, out, preferred_element_type=jnp.float32)
    back = jnp.where(allowed, jnp.exp(scores - log_total), 0.0)
    value_grad = jnp.einsum(
        "chrs,rchd->schd", back.astype(jnp.bfloat16), grad, preferred_element_type=jnp.float32
    )
    prob_grad = jnp.einsum("rchd,schd->chrs", grad, v, preferred_element_type=jnp.float32)
    score_grad = (back * (prob_grad - grad_dot[..., None])).astype(jnp.bfloat16)
    query_grad = jnp.einsum("chrs,schd->rchd", score_grad, k, preferred_element_type=jnp.float32)
    key_grad = jnp.einsum("chrs,rchd->schd", score_grad, q, preferred_element_type=jnp.float32)
    return tuple(
        g.astype(jnp.bfloat16) for g in (query_grad * scale, key_grad * scale, value_grad)
    )


def on_device(queries, keys, values, out_grad, out_weight, row_mask, col_mask):
    tokens, features = queries.shape[2], queries.shape[3]
    half = features // 2
    heads_half = half // DH
    rows = lax.axis_size("seq")
    cols_each = tokens // rows

    weight = lax.all_gather(out_weight, "dp", axis=0, tiled=True)

    bounds = [0, cols_each * 3 // 4, cols_each]
    chunks = len(bounds) - 1
    widths = [bounds[j + 1] - bounds[j] for j in range(chunks)]

    def chunked(t):
        by_dest = t.reshape(rows, cols_each, half)
        return [by_dest[:, bounds[j] : bounds[j + 1]] for j in range(chunks)]

    col_in = [chunked(t[0, 0, :, half:]) for t in (queries, keys, values)]
    col_ok = col_mask == 1
    shipped_all = [
        lax.all_to_all(
            jnp.stack([part[j] for part in col_in]), "seq", split_axis=1, concat_axis=1, tiled=True
        )
        for j in range(chunks)
    ]

    row_ok = row_permit(row_mask)
    split = lambda t: t[0, 0, :, :half].reshape(tokens, heads_half, DH)
    row_q, row_k, row_v = split(queries), split(keys), split(values)
    row_out, row_scores, row_total = row_forward(row_q, row_k, row_v, row_ok)
    row_attn = row_out.reshape(tokens, half)
    flat_grad = out_grad[0, 0]
    contract = (((0,), (0,)), ((), ()))
    row_done, shipped_first = lax.optimization_barrier(
        ((row_out, row_scores, row_total), shipped_all[0])
    )
    row_out, row_scores, row_total = row_done
    row_attn = row_out.reshape(tokens, half)
    shipped_all[0] = shipped_first

    col_state = []
    col_back = []
    for j in range(chunks):
        shipped = shipped_all[j]
        if j > 0:
            done_before, shipped = lax.optimization_barrier((col_state[j - 1], shipped))
            col_state[j - 1] = done_before
            col_back[j - 1] = done_before[3].reshape(rows, widths[j - 1], half)
        col_q, col_k, col_v = (
            shipped[i].reshape(rows, widths[j], heads_half, DH) for i in range(3)
        )
        col_out, col_scores, col_total = column_forward(col_q, col_k, col_v, col_ok)
        col_state.append((col_q, col_k, col_v, col_out, col_scores, col_total))
        col_back.append(col_out.reshape(rows, widths[j], half))
    col_attn = lax.all_to_all(
        jnp.concatenate(col_back, axis=1), "seq", split_axis=0, concat_axis=0, tiled=True
    ).reshape(tokens, half)

    attention = jnp.concatenate([row_attn, col_attn], axis=1)
    partial = lax.dot_general(attention, flat_grad, contract, preferred_element_type=jnp.float32)

    by_rows_of = (((1,), (1,)), ((), ()))
    row_grad = lax.dot_general(
        flat_grad, weight[:half], by_rows_of, preferred_element_type=jnp.float32
    ).astype(jnp.bfloat16)
    partial, late_weight = lax.optimization_barrier((partial, weight))
    col_grad = lax.dot_general(
        flat_grad, late_weight[half:], by_rows_of, preferred_element_type=jnp.float32
    ).astype(jnp.bfloat16)
    back_bounds = [0, cols_each // 2, cols_each]
    by_dest = col_grad.reshape(rows, cols_each, half)
    grad_col_part = [by_dest[:, back_bounds[j] : back_bounds[j + 1]] for j in range(2)]
    whole_state = [
        jnp.concatenate([st[i] for st in col_state], axis=1 if i < 4 else 0) for i in range(6)
    ]
    col_state = [
        tuple(
            t[:, back_bounds[j] : back_bounds[j + 1]] if i < 4 else t[back_bounds[j] : back_bounds[j + 1]]
            for i, t in enumerate(whole_state)
        )
        for j in range(2)
    ]
    widths = [back_bounds[j + 1] - back_bounds[j] for j in range(2)]
    devices_all = lax.axis_size(("dp", "seq"))
    wo_grad = lax.psum_scatter(
        partial.astype(jnp.bfloat16), ("dp", "seq"), scatter_dimension=0, tiled=True
    ).astype(jnp.float32) * (1.0 / math.sqrt(tokens * devices_all))

    col_grads_back = []
    for j in range(2):
        grad_cols = lax.all_to_all(
            grad_col_part[j], "seq", split_axis=0, concat_axis=0, tiled=True
        ).reshape(rows, widths[j], heads_half, DH)
        col_q, col_k, col_v, col_out, col_scores, col_total = col_state[j]
        col_grads = column_backward(
            col_q, col_k, col_v, col_out, grad_cols, col_scores, col_total, col_ok
        )
        col_grads_back.append(
            lax.all_to_all(
                jnp.stack([g.reshape(rows, widths[j], half) for g in col_grads]),
                "seq",
                split_axis=1,
                concat_axis=1,
                tiled=True,
            )
        )
    col_grads_whole = jnp.concatenate(col_grads_back, axis=2).reshape(3, tokens, half)

    row_grads = row_backward(
        row_q,
        row_k,
        row_v,
        row_out,
        row_grad.reshape(tokens, heads_half, DH),
        row_scores,
        row_total,
        row_ok,
    )

    layer_out = jnp.dot(attention, weight, preferred_element_type=jnp.float32).astype(
        jnp.bfloat16
    )

    grads = [
        jnp.concatenate([row_grads[i].reshape(tokens, half), col_grads_whole[i]], axis=1)[
            None, None
        ]
        for i in range(3)
    ]
    return (layer_out[None, None], grads[0], grads[1], grads[2], wo_grad)


def solution(mesh):
    in_specs = (
        P("dp", "seq", None, None),
        P("dp", "seq", None, None),
        P("dp", "seq", None, None),
        P("dp", "seq", None, None),
        P("dp", None),
        P(),
        P(),
    )
    out_specs = (
        P("dp", "seq", None, None),
        P("dp", "seq", None, None),
        P("dp", "seq", None, None),
        P("dp", "seq", None, None),
        P(("dp", "seq"), None),
    )
    return jax.shard_map(
        on_device, mesh=mesh, in_specs=in_specs, out_specs=out_specs, check_vma=False
    )
```

```python
import math

import jax
import jax.numpy as jnp
from jax import lax
from jax.sharding import PartitionSpec as P

DH = 128
COLS = 512
BLK = 128

masked_out = -1e30
scale = 1.0 / math.sqrt(DH)


def row_permit(row_mask):
    spread = jnp.repeat(jnp.repeat(row_mask, BLK, axis=0), BLK, axis=1)
    row_index = lax.broadcasted_iota(jnp.int32, (COLS, COLS), 0)
    col_index = lax.broadcasted_iota(jnp.int32, (COLS, COLS), 1)
    return (spread == 1) & (col_index <= row_index)


def softmax_parts(scores, allowed):
    highest = jnp.max(jnp.where(allowed, scores, masked_out), axis=-1, keepdims=True)
    attend = jnp.exp(jnp.where(allowed, scores - highest, masked_out))
    totals = jnp.sum(attend, axis=-1, keepdims=True)
    probs = (attend / totals).astype(jnp.bfloat16)
    return probs, highest + jnp.log(totals)


def row_forward(q, k, v, allowed):
    scores = jnp.einsum("ihd,jhd->hij", q, k, preferred_element_type=jnp.float32) * scale
    probs, log_total = softmax_parts(scores, allowed[None])
    out = jnp.einsum("hij,jhd->ihd", probs, v, preferred_element_type=jnp.float32)
    return out.astype(jnp.bfloat16), scores, log_total


def row_backward(q, k, v, out, grad, scores, log_total, allowed):
    grad_dot = jnp.einsum("ihd,ihd->hi", grad, out, preferred_element_type=jnp.float32)
    back = jnp.where(allowed[None], jnp.exp(scores - log_total), 0.0)
    value_grad = jnp.einsum(
        "hij,ihd->jhd", back.astype(jnp.bfloat16), grad, preferred_element_type=jnp.float32
    )
    prob_grad = jnp.einsum("ihd,jhd->hij", grad, v, preferred_element_type=jnp.float32)
    score_grad = (back * (prob_grad - grad_dot[..., None])).astype(jnp.bfloat16)
    query_grad = jnp.einsum("hij,jhd->ihd", score_grad, k, preferred_element_type=jnp.float32)
    key_grad = jnp.einsum("hij,ihd->jhd", score_grad, q, preferred_element_type=jnp.float32)
    return tuple(
        g.astype(jnp.bfloat16) for g in (query_grad * scale, key_grad * scale, value_grad)
    )


def column_forward(q, k, v, allowed):
    scores = jnp.einsum("rchd,schd->chrs", q, k, preferred_element_type=jnp.float32) * scale
    probs, log_total = softmax_parts(scores, allowed)
    out = jnp.einsum("chrs,schd->rchd", probs, v, preferred_element_type=jnp.float32)
    return out.astype(jnp.bfloat16), scores, log_total


def column_backward(q, k, v, out, grad, scores, log_total, allowed):
    grad_dot = jnp.einsum("rchd,rchd->chr", grad, out, preferred_element_type=jnp.float32)
    back = jnp.where(allowed, jnp.exp(scores - log_total), 0.0)
    value_grad = jnp.einsum(
        "chrs,rchd->schd", back.astype(jnp.bfloat16), grad, preferred_element_type=jnp.float32
    )
    prob_grad = jnp.einsum("rchd,schd->chrs", grad, v, preferred_element_type=jnp.float32)
    score_grad = (back * (prob_grad - grad_dot[..., None])).astype(jnp.bfloat16)
    query_grad = jnp.einsum("chrs,schd->rchd", score_grad, k, preferred_element_type=jnp.float32)
    key_grad = jnp.einsum("chrs,rchd->schd", score_grad, q, preferred_element_type=jnp.float32)
    return tuple(
        g.astype(jnp.bfloat16) for g in (query_grad * scale, key_grad * scale, value_grad)
    )


def on_device(queries, keys, values, out_grad, out_weight, row_mask, col_mask):
    tokens, features = queries.shape[2], queries.shape[3]
    half = features // 2
    heads_half = half // DH
    rows = lax.axis_size("seq")
    cols_each = tokens // rows

    weight = lax.all_gather(out_weight, "dp", axis=0, tiled=True)

    chunks = 2
    piece = cols_each // chunks

    def chunked(t):
        return t.reshape(rows, chunks, piece, half).transpose(1, 0, 2, 3)

    packed = jnp.stack([chunked(t[0, 0, :, half:]) for t in (queries, keys, values)], axis=1)
    col_ok = col_mask == 1
    shipped_all = [
        lax.all_to_all(packed[j], "seq", split_axis=1, concat_axis=1, tiled=True)
        for j in range(chunks)
    ]

    row_ok = row_permit(row_mask)
    split = lambda t: t[0, 0, :, :half].reshape(tokens, heads_half, DH)
    row_q, row_k, row_v = split(queries), split(keys), split(values)
    row_out, row_scores, row_total = row_forward(row_q, row_k, row_v, row_ok)
    row_attn = row_out.reshape(tokens, half)
    flat_grad = out_grad[0, 0]
    contract = (((0,), (0,)), ((), ()))
    row_done, shipped_first = lax.optimization_barrier(
        ((row_out, row_scores, row_total), shipped_all[0])
    )
    row_out, row_scores, row_total = row_done
    row_attn = row_out.reshape(tokens, half)
    shipped_all[0] = shipped_first

    col_state = []
    col_back = []
    for j in range(chunks):
        shipped = shipped_all[j]
        if j > 0:
            done_before, shipped = lax.optimization_barrier((col_state[j - 1], shipped))
            col_state[j - 1] = done_before
            col_back[j - 1] = done_before[3].reshape(rows, piece, half)
        col_q, col_k, col_v = (
            shipped[i].reshape(rows, piece, heads_half, DH) for i in range(3)
        )
        col_out, col_scores, col_total = column_forward(col_q, col_k, col_v, col_ok)
        col_state.append((col_q, col_k, col_v, col_out, col_scores, col_total))
        col_back.append(col_out.reshape(rows, piece, half))
    col_attn = lax.all_to_all(
        jnp.stack(col_back, axis=1), "seq", split_axis=0, concat_axis=0, tiled=True
    ).reshape(tokens, half)

    attention = jnp.concatenate([row_attn, col_attn], axis=1)
    partial = lax.dot_general(attention, flat_grad, contract, preferred_element_type=jnp.bfloat16)

    by_rows_of = (((1,), (1,)), ((), ()))
    row_grad = lax.dot_general(
        flat_grad, weight[:half], by_rows_of, preferred_element_type=jnp.float32
    ).astype(jnp.bfloat16)
    partial, late_weight = lax.optimization_barrier((partial, weight))
    col_grad = lax.dot_general(
        flat_grad, late_weight[half:], by_rows_of, preferred_element_type=jnp.float32
    ).astype(jnp.bfloat16)
    grad_col_part = chunked(col_grad)
    devices_all = lax.axis_size(("dp", "seq"))
    wo_grad = lax.psum_scatter(
        partial, ("dp", "seq"), scatter_dimension=0, tiled=True
    ).astype(jnp.float32) * (1.0 / math.sqrt(tokens * devices_all))

    col_grads_back = []
    for j in range(chunks):
        grad_cols = lax.all_to_all(
            grad_col_part[j], "seq", split_axis=0, concat_axis=0, tiled=True
        ).reshape(rows, piece, heads_half, DH)
        col_q, col_k, col_v, col_out, col_scores, col_total = col_state[j]
        col_grads = column_backward(
            col_q, col_k, col_v, col_out, grad_cols, col_scores, col_total, col_ok
        )
        col_grads_back.append(
            lax.all_to_all(
                jnp.stack([g.reshape(rows, piece, half) for g in col_grads]),
                "seq",
                split_axis=1,
                concat_axis=1,
                tiled=True,
            )
        )
    col_grads_whole = jnp.stack(col_grads_back, axis=2).reshape(3, tokens, half)

    row_grads = row_backward(
        row_q,
        row_k,
        row_v,
        row_out,
        row_grad.reshape(tokens, heads_half, DH),
        row_scores,
        row_total,
        row_ok,
    )

    layer_out = jnp.dot(attention, weight, preferred_element_type=jnp.float32).astype(
        jnp.bfloat16
    )

    grads = [
        jnp.concatenate([row_grads[i].reshape(tokens, half), col_grads_whole[i]], axis=1)[
            None, None
        ]
        for i in range(3)
    ]
    return (layer_out[None, None], grads[0], grads[1], grads[2], wo_grad)


def solution(mesh):
    in_specs = (
        P("dp", "seq", None, None),
        P("dp", "seq", None, None),
        P("dp", "seq", None, None),
        P("dp", "seq", None, None),
        P("dp", None),
        P(),
        P(),
    )
    out_specs = (
        P("dp", "seq", None, None),
        P("dp", "seq", None, None),
        P("dp", "seq", None, None),
        P("dp", "seq", None, None),
        P(("dp", "seq"), None),
    )
    return jax.shard_map(
        on_device, mesh=mesh, in_specs=in_specs, out_specs=out_specs, check_vma=False
    )
```

```python
import math

import jax
import jax.numpy as jnp
from jax import lax
from jax.sharding import PartitionSpec as P

DH = 128
COLS = 512
BLK = 128

masked_out = -1e30
scale = 1.0 / math.sqrt(DH)


def row_permit(row_mask):
    spread = jnp.repeat(jnp.repeat(row_mask, BLK, axis=0), BLK, axis=1)
    row_index = lax.broadcasted_iota(jnp.int32, (COLS, COLS), 0)
    col_index = lax.broadcasted_iota(jnp.int32, (COLS, COLS), 1)
    return (spread == 1) & (col_index <= row_index)


def softmax_parts(scores, allowed):
    highest = jnp.max(jnp.where(allowed, scores, masked_out), axis=-1, keepdims=True)
    attend = jnp.exp(jnp.where(allowed, scores - highest, masked_out))
    totals = jnp.sum(attend, axis=-1, keepdims=True)
    probs = (attend / totals).astype(jnp.bfloat16)
    return probs, highest + jnp.log(totals)


def row_forward(q, k, v, allowed):
    scores = jnp.einsum("ihd,jhd->hij", q, k, preferred_element_type=jnp.float32) * scale
    probs, log_total = softmax_parts(scores, allowed[None])
    out = jnp.einsum("hij,jhd->ihd", probs, v, preferred_element_type=jnp.float32)
    return out.astype(jnp.bfloat16), scores, log_total


def row_backward(q, k, v, out, grad, scores, log_total, allowed):
    grad_dot = jnp.einsum("ihd,ihd->hi", grad, out, preferred_element_type=jnp.float32)
    back = jnp.where(allowed[None], jnp.exp(scores - log_total), 0.0)
    value_grad = jnp.einsum(
        "hij,ihd->jhd", back.astype(jnp.bfloat16), grad, preferred_element_type=jnp.float32
    )
    prob_grad = jnp.einsum("ihd,jhd->hij", grad, v, preferred_element_type=jnp.float32)
    score_grad = (back * (prob_grad - grad_dot[..., None])).astype(jnp.bfloat16)
    query_grad = jnp.einsum("hij,jhd->ihd", score_grad, k, preferred_element_type=jnp.float32)
    key_grad = jnp.einsum("hij,ihd->jhd", score_grad, q, preferred_element_type=jnp.float32)
    return tuple(
        g.astype(jnp.bfloat16) for g in (query_grad * scale, key_grad * scale, value_grad)
    )


def column_forward(q, k, v, allowed):
    scores = jnp.einsum("rchd,schd->chrs", q, k, preferred_element_type=jnp.float32) * scale
    probs, log_total = softmax_parts(scores, allowed)
    out = jnp.einsum("chrs,schd->rchd", probs, v, preferred_element_type=jnp.float32)
    return out.astype(jnp.bfloat16), scores, log_total


def column_backward(q, k, v, out, grad, scores, log_total, allowed):
    grad_dot = jnp.einsum("rchd,rchd->chr", grad, out, preferred_element_type=jnp.float32)
    back = jnp.where(allowed, jnp.exp(scores - log_total), 0.0)
    value_grad = jnp.einsum(
        "chrs,rchd->schd", back.astype(jnp.bfloat16), grad, preferred_element_type=jnp.float32
    )
    prob_grad = jnp.einsum("rchd,schd->chrs", grad, v, preferred_element_type=jnp.float32)
    score_grad = (back * (prob_grad - grad_dot[..., None])).astype(jnp.bfloat16)
    query_grad = jnp.einsum("chrs,schd->rchd", score_grad, k, preferred_element_type=jnp.float32)
    key_grad = jnp.einsum("chrs,rchd->schd", score_grad, q, preferred_element_type=jnp.float32)
    return tuple(
        g.astype(jnp.bfloat16) for g in (query_grad * scale, key_grad * scale, value_grad)
    )


def on_device(queries, keys, values, out_grad, out_weight, row_mask, col_mask):
    tokens, features = queries.shape[2], queries.shape[3]
    half = features // 2
    heads_half = half // DH
    rows = lax.axis_size("seq")
    cols_each = tokens // rows

    weight = lax.all_gather(out_weight, "dp", axis=0, tiled=True)

    chunks = 2
    piece = cols_each // chunks

    def chunked(t):
        return t.reshape(rows, chunks, piece, half).transpose(1, 0, 2, 3)

    col_in = [chunked(t[0, 0, :, half:]) for t in (queries, keys, values)]
    col_ok = col_mask == 1
    shipped_all = [
        lax.all_to_all(
            jnp.stack([part[j] for part in col_in]), "seq", split_axis=1, concat_axis=1, tiled=True
        )
        for j in range(chunks)
    ]

    row_ok = row_permit(row_mask)
    split = lambda t: t[0, 0, :, :half].reshape(tokens, heads_half, DH)
    row_q, row_k, row_v = split(queries), split(keys), split(values)
    row_out, row_scores, row_total = row_forward(row_q, row_k, row_v, row_ok)
    row_attn = row_out.reshape(tokens, half)
    flat_grad = out_grad[0, 0]
    contract = (((0,), (0,)), ((), ()))
    row_done, shipped_first = lax.optimization_barrier(
        ((row_out, row_scores, row_total), shipped_all[0])
    )
    row_out, row_scores, row_total = row_done
    row_attn = row_out.reshape(tokens, half)
    shipped_all[0] = shipped_first

    col_state = []
    col_back = []
    for j in range(chunks):
        shipped = shipped_all[j]
        if j > 0:
            done_before, shipped = lax.optimization_barrier((col_state[j - 1], shipped))
            col_state[j - 1] = done_before
            col_back[j - 1] = done_before[3].reshape(rows, piece, half)
        col_q, col_k, col_v = (
            shipped[i].reshape(rows, piece, heads_half, DH) for i in range(3)
        )
        col_out, col_scores, col_total = column_forward(col_q, col_k, col_v, col_ok)
        col_state.append((col_q, col_k, col_v, col_out, col_scores, col_total))
        col_back.append(col_out.reshape(rows, piece, half))
    col_attn = lax.all_to_all(
        jnp.stack(col_back, axis=1), "seq", split_axis=0, concat_axis=0, tiled=True
    ).reshape(tokens, half)

    attention = jnp.concatenate([row_attn, col_attn], axis=1)
    partial = lax.dot_general(attention, flat_grad, contract, preferred_element_type=jnp.float32)

    by_rows_of = (((1,), (1,)), ((), ()))
    row_grad = lax.dot_general(
        flat_grad, weight[:half], by_rows_of, preferred_element_type=jnp.float32
    ).astype(jnp.bfloat16)
    partial, late_weight = lax.optimization_barrier((partial, weight))
    col_grad = lax.dot_general(
        flat_grad, late_weight[half:], by_rows_of, preferred_element_type=jnp.float32
    ).astype(jnp.bfloat16)
    grad_col_part = chunked(col_grad)
    devices_all = lax.axis_size(("dp", "seq"))
    wo_grad = lax.psum_scatter(
        partial.astype(jnp.bfloat16), ("dp", "seq"), scatter_dimension=0, tiled=True
    ).astype(jnp.float32) * (1.0 / math.sqrt(tokens * devices_all))

    col_grads_back = []
    for j in range(chunks):
        grad_cols = lax.all_to_all(
            grad_col_part[j], "seq", split_axis=0, concat_axis=0, tiled=True
        ).reshape(rows, piece, heads_half, DH)
        col_q, col_k, col_v, col_out, col_scores, col_total = col_state[j]
        col_grads = column_backward(
            col_q, col_k, col_v, col_out, grad_cols, col_scores, col_total, col_ok
        )
        col_grads_back.append(
            lax.all_to_all(
                jnp.stack([g.reshape(rows, piece, half) for g in col_grads]),
                "seq",
                split_axis=1,
                concat_axis=1,
                tiled=True,
            )
        )
    col_grads_whole = jnp.stack(col_grads_back, axis=2).reshape(3, tokens, half)

    row_grads = row_backward(
        row_q,
        row_k,
        row_v,
        row_out,
        row_grad.reshape(tokens, heads_half, DH),
        row_scores,
        row_total,
        row_ok,
    )

    layer_out = jnp.dot(attention, weight, preferred_element_type=jnp.float32).astype(
        jnp.bfloat16
    )

    grads = [
        jnp.concatenate([row_grads[i].reshape(tokens, half), col_grads_whole[i]], axis=1)[
            None, None
        ]
        for i in range(3)
    ]
    return (layer_out[None, None], grads[0], grads[1], grads[2], wo_grad)


def solution(mesh):
    in_specs = (
        P("dp", "seq", None, None),
        P("dp", "seq", None, None),
        P("dp", "seq", None, None),
        P("dp", "seq", None, None),
        P("dp", None),
        P(),
        P(),
    )
    out_specs = (
        P("dp", "seq", None, None),
        P("dp", "seq", None, None),
        P("dp", "seq", None, None),
        P("dp", "seq", None, None),
        P(("dp", "seq"), None),
    )
    return jax.shard_map(
        on_device, mesh=mesh, in_specs=in_specs, out_specs=out_specs, check_vma=False
    )
```
